512 devices in a mesh: seq: 64 (over z, y), chan: 8 (over x, core).
Axes of the slice: x: 4, y: 8, z: 8, core: 2. Of those that a mesh axis runs over, the one named last changes fastest.
Arguments:
- tokens: bfloat16 [8192, 4096], P('seq', 'chan'), may hold values from -6 to 6
- conv_taps: float32 [4, 4096], P(None, 'chan'), may hold values from -12 to 12
- log_rate: float32 [4096], P('chan'), may hold values from 4.8828125e-06 to 0.034
- rotation: float32 [4096], P('chan'), may hold values from 0 to 0.2
- in_proj: bfloat16 [64, 64, 128], P('chan'), may hold values from -0.75 to 0.75
- out_proj: bfloat16 [64, 64, 128], P('chan'), may hold values from -0.5 to 0.5
- skip_gain: float32 [4096], P('chan'), may hold values from 0.25 to 1.5
- norm_gain: float32 [4096], P('chan'), may hold values from 0.25 to 1.75
- retention: float32 [8192], P('seq'), may hold values from 0.5 to 1
- cotangent: bfloat16 [8192, 4096], P('seq', 'chan'), may hold values from -6 to 6
Outputs:
- normed: bfloat16 [8192, 4096], P('seq', 'chan')
- tokens_grad: bfloat16 [8192, 4096], P('seq', 'chan')
- in_grad: float32 [64, 64, 128], P('chan')
- out_grad: float32 [64, 64, 128], P('chan')
- taps_grad: float32 [4, 4096], P(None, 'chan')
The draws below stay inside these ranges and needn't reach their ends.
All inputs are finite; a program needn't handle non-finite values.
Results may differ from the reference program's by a relative error of at most 0.011.
Values may be sent and summed in bfloat16 or wider, within the bound.
No kernel may reach another device: no remote copies, remote signals or barrier semaphores. Data moves between devices by JAX's collectives and lax.ppermute only.
A program may use at most 64 MiB of HBM per device.

```python
import jax
import jax.numpy as jnp
from jax import lax

D = 4096
HW = 64
STATE = 64
KW = 4
TOK_DEV = 128
HEADS = 64
STATES = 4096
TOKENS = 8192


def draw_conv_taps(key, part):
    first_key, second_key = jax.random.split(key)
    channels = jnp.arange(D, dtype=jnp.float32)
    rising = jnp.exp(0.5 * jnp.log(3.0) * channels / D)
    jitter = jnp.exp(jax.random.uniform(second_key, (D,), jnp.float32, jnp.log(0.3), jnp.log(3.0)))
    base = jnp.clip(jax.random.normal(first_key, (KW, D), jnp.float32), -4.0, 4.0)
    return 0.5 * base * rising[None, :] * jitter[None, :]


def draw_log_rate(key, part):
    first_key, second_key, third_key = jax.random.split(key, 3)
    slow_flag = jax.random.randint(first_key, (STATES,), 0, 2) > 0
    slow_rate = jnp.exp(jax.random.uniform(second_key, (STATES,), jnp.float32, jnp.log(0.05), jnp.log(2.0))) / TOKENS
    fast_rate = jnp.exp(jax.random.uniform(third_key, (STATES,), jnp.float32, jnp.log(1.0 / 50.0), jnp.log(1.0 / 30.0)))
    return jnp.where(slow_flag, slow_rate, fast_rate)


def draw_retention(key, part):
    first_key, second_key = jax.random.split(key)
    hits = jax.random.randint(first_key, (TOKENS,), 0, TOKENS) < 12
    dropped = jax.random.uniform(second_key, (TOKENS,), jnp.float32, 0.5, 0.8)
    return jnp.where(hits, dropped, 1.0)


def block_scale(rng, extent, cuts, low, largest):
    gain = 1.0
    for position, parts in cuts:
        draws = jax.random.uniform(jax.random.fold_in(jax.random.fold_in(rng, 6), position), (parts,), jnp.float32, low / len(cuts), largest / len(cuts))
        gain = gain * jnp.repeat(jnp.exp(draws), extent[position] // parts).reshape((-1,) + (1,) * (len(extent) - 1 - position))
    return gain


def gaussian(stream_key, shape, scale, bound, shards=(), kind=jnp.bfloat16):
    result = scale * jax.random.normal(stream_key, shape, jnp.float32)
    if shards:
        result = result * block_scale(stream_key, shape, shards, -0.22, 0.18)
    return jnp.clip(result, -bound, bound).astype(kind)


def setup_inputs(seed: int = 0) -> dict:
    arg_keys = jax.random.split(jax.random.key(seed), 11)
    return {
        "tokens": gaussian(arg_keys[0], (TOKENS, D), 1.0, 6.0, ((0, 64), (1, 8))),
        "conv_taps": draw_conv_taps(jax.random.fold_in(arg_keys[10], 71), 0),
        "log_rate": draw_log_rate(jax.random.fold_in(arg_keys[10], 71), 0),
        "rotation": jnp.clip(0.2 * jax.random.uniform(arg_keys[3], (STATES,), jnp.float32) ** block_scale(arg_keys[3], (STATES,), ((0, 8),), -0.2, 0.2), 0.0, 0.2),
        "in_proj": gaussian(arg_keys[4], (HEADS, HW, 2 * STATE), HW ** -0.5, 0.75, ((0, 8),)),
        "out_proj": gaussian(arg_keys[5], (HEADS, HW, 2 * STATE), (2 * STATE) ** -0.5, 0.5, ((0, 8),)),
        "skip_gain": jnp.clip(0.25 + 1.25 * jax.random.uniform(arg_keys[6], (D,), jnp.float32) ** block_scale(arg_keys[6], (D,), ((0, 8),), -0.2, 0.2), 0.25, 1.5),
        "norm_gain": jnp.clip(1.0 + 0.15 * jax.random.normal(arg_keys[7], (D,), jnp.float32), 0.25, 1.75),
        "retention": draw_retention(jax.random.fold_in(arg_keys[10], 71), 0),
        "cotangent": gaussian(arg_keys[9], (TOKENS, D), 1.0, 6.0, ((0, 64), (1, 8))),
    }


def reference(tokens, conv_taps, log_rate, rotation, in_proj, out_proj, skip_gain, norm_gain, retention, cotangent):
    block_total = TOKENS // TOK_DEV
    decay_mag = jnp.exp(-log_rate)
    lam_re = decay_mag * jnp.cos(rotation)
    lam_im = decay_mag * jnp.sin(rotation)
    in_scale = jnp.sqrt(-jnp.expm1(-2.0 * log_rate))
    in_wide = in_proj.astype(jnp.float32)
    out_wide = out_proj.astype(jnp.float32)
    token_blocks = tokens.reshape(block_total, TOK_DEV, D)
    keep_blocks = retention.reshape(block_total, TOK_DEV)
    cot_blocks = cotangent.reshape(block_total, TOK_DEV, D)
    highest = lax.Precision.HIGHEST

    def convolve(block, lead_rows):
        padded = jnp.concatenate([lead_rows, block.astype(jnp.float32)], axis=0)
        summed = conv_taps[0][None, :] * padded[KW - 1:]
        for offset in range(1, KW):
            summed = summed + conv_taps[offset][None, :] * padded[KW - 1 - offset:KW - 1 - offset + TOK_DEV]
        return (summed.astype(jnp.bfloat16), padded)

    def drive(mixed_in):
        projected = jnp.einsum('thc,hck->thk', mixed_in.astype(jnp.float32).reshape(TOK_DEV, HEADS, HW), in_wide, precision=highest)
        drive_re = projected[:, :, :STATE].reshape(TOK_DEV, STATES) * in_scale
        drive_im = projected[:, :, STATE:].reshape(TOK_DEV, STATES) * in_scale
        return (drive_re, drive_im)

    def states(start_re, start_im, drive_re, drive_im, keep):

        def advance(carried, item):
            old_re, old_im = carried
            in_re, in_im, keep_now = item
            new_re = keep_now * (lam_re * old_re - lam_im * old_im) + in_re
            new_im = keep_now * (lam_re * old_im + lam_im * old_re) + in_im
            return ((new_re, new_im), (new_re, new_im))
        return lax.scan(advance, (start_re, start_im), (drive_re, drive_im, keep))[1]

    def readout(seq_re, seq_im, mixed_in):
        state_bf = jnp.concatenate([seq_re.reshape(TOK_DEV, HEADS, STATE), seq_im.reshape(TOK_DEV, HEADS, STATE)], axis=2).astype(jnp.bfloat16)
        mixed = jnp.einsum('thk,hck->thc', state_bf.astype(jnp.float32), out_wide, precision=highest).reshape(TOK_DEV, D)
        mixed = mixed + skip_gain * mixed_in.astype(jnp.float32)
        return (state_bf, mixed)

    def forward_step(carried, item):
        start_re, start_im, lead_rows = carried
        block, keep = item
        mixed_in, padded = convolve(block, lead_rows)
        drive_re, drive_im = drive(mixed_in)
        seq_re, seq_im = states(start_re, start_im, drive_re, drive_im, keep)
        state_bf, mixed = readout(seq_re, seq_im, mixed_in)
        inverse = lax.rsqrt(lax.optimization_barrier(jnp.mean(mixed * mixed, axis=1)) + 1e-06)
        normed = (mixed * inverse[:, None] * norm_gain).astype(jnp.bfloat16)
        return ((seq_re[-1], seq_im[-1], padded[TOK_DEV:]), (normed, start_re, start_im, lead_rows))
    zero_state = jnp.zeros((STATES,), jnp.float32)
    zero_lead = jnp.zeros((KW - 1, D), jnp.float32)
    normed_blocks, starts_re, starts_im, leads = lax.scan(forward_step, (zero_state, zero_state, zero_lead), (token_blocks, keep_blocks))[1]

    def backward_step(carried, item):
        pend_re, pend_im, trail_rows, in_acc, out_acc, taps_acc = carried
        block, keep, cot, start_re, start_im, lead_rows = item
        mixed_in, padded = convolve(block, lead_rows)
        drive_re, drive_im = drive(mixed_in)
        seq_re, seq_im = states(start_re, start_im, drive_re, drive_im, keep)
        state_bf, mixed = readout(seq_re, seq_im, mixed_in)
        inverse = lax.rsqrt(lax.optimization_barrier(jnp.mean(mixed * mixed, axis=1)) + 1e-06)
        scaled = cot.astype(jnp.float32) * norm_gain
        dots = lax.optimization_barrier(jnp.sum(scaled * mixed, axis=1))
        mixed_grad = inverse[:, None] * (scaled - mixed * (inverse * inverse * dots / D)[:, None])
        grad_bf = mixed_grad.astype(jnp.bfloat16).reshape(TOK_DEV, HEADS, HW).astype(jnp.float32)
        state_grad = jnp.einsum('thc,hck->thk', grad_bf, out_wide, precision=highest)
        out_acc = out_acc + jnp.einsum('thc,thk->hck', grad_bf, state_bf.astype(jnp.float32), precision=highest)

        def retreat(pending, item_now):
            pending_re, pending_im = pending
            grad_re, grad_im, keep_now = item_now
            adj_re = grad_re + pending_re
            adj_im = grad_im + pending_im
            next_re = keep_now * (lam_re * adj_re + lam_im * adj_im)
            next_im = keep_now * (lam_re * adj_im - lam_im * adj_re)
            return ((next_re, next_im), (adj_re, adj_im))
        grad_re = state_grad[:, :, :STATE].reshape(TOK_DEV, STATES)
        grad_im = state_grad[:, :, STATE:].reshape(TOK_DEV, STATES)
        (pend_re, pend_im), (adj_re, adj_im) = lax.scan(retreat, (pend_re, pend_im), (grad_re, grad_im, keep), reverse=True)
        drive_grad = jnp.concatenate([(in_scale * adj_re).reshape(TOK_DEV, HEADS, STATE), (in_scale * adj_im).reshape(TOK_DEV, HEADS, STATE)], axis=2).astype(jnp.bfloat16).astype(jnp.float32)
        in_acc = in_acc + jnp.einsum('thc,thk->hck', mixed_in.astype(jnp.float32).reshape(TOK_DEV, HEADS, HW), drive_grad, precision=highest)
        input_grad = jnp.einsum('thk,hck->thc', drive_grad, in_wide, precision=highest).reshape(TOK_DEV, D) + skip_gain * mixed_grad
        tail = jnp.concatenate([input_grad, trail_rows], axis=0)
        grad_tokens = conv_taps[0][None, :] * tail[:TOK_DEV]
        for offset in range(1, KW):
            grad_tokens = grad_tokens + conv_taps[offset][None, :] * tail[offset:offset + TOK_DEV]
        taps_term = jnp.stack([lax.optimization_barrier(jnp.sum(input_grad * padded[KW - 1 - offset:KW - 1 - offset + TOK_DEV], axis=0)) for offset in range(KW)])
        taps_acc = taps_acc + taps_term
        return ((pend_re, pend_im, input_grad[:KW - 1], in_acc, out_acc, taps_acc), grad_tokens.astype(jnp.bfloat16))
    zero_proj = jnp.zeros((HEADS, HW, 2 * STATE), jnp.float32)
    zero_taps = jnp.zeros((KW, D), jnp.float32)
    init = (zero_state, zero_state, zero_lead, zero_proj, zero_proj, zero_taps)
    final, grad_blocks = lax.scan(backward_step, init, (token_blocks, keep_blocks, cot_blocks, starts_re, starts_im, leads), reverse=True)
    return (normed_blocks.reshape(TOKENS, D), grad_blocks.reshape(TOKENS, D), final[3], final[4], final[5])
```

```python
import jax
import jax.numpy as jnp
from jax import lax
from jax.sharding import PartitionSpec as P


def from_behind(value, axis, by):
    length = lax.axis_size(axis)
    pairs = [(i, i + by) for i in range(length) if 0 <= i + by < length]
    return lax.ppermute(value, axis, pairs)


def carried_in(part, axis, combine, identity, reverse):
    count = lax.axis_size(axis)
    place = lax.axis_index(axis)
    ahead = count - 1 - place if reverse else place
    step = -1 if reverse else 1
    packed = jnp.stack(part)
    unit = jnp.stack([jnp.zeros_like(a) + jnp.asarray(e, a.dtype) for a, e in zip(part, identity)])
    state = jnp.where(ahead >= 1, from_behind(packed, axis, step), unit)
    reach = 1
    while reach < count:
        earlier = from_behind(state, axis, step * reach)
        joined = jnp.stack(combine(tuple(earlier), tuple(state)))
        state = jnp.where(ahead >= reach, joined, state)
        reach *= 2
    return tuple(state)


def linear_run(drive_re, drive_im, decay_rate, turn_rate, log_keep):
    seq_len, num_cols = drive_re.shape
    block_len = min(64, seq_len)
    block_count = seq_len // block_len
    offsets = jnp.arange(block_len, dtype=jnp.float32)
    keep_cum = jnp.cumsum(log_keep.reshape(block_count, block_len), axis=1)[:, :, None]
    angles = offsets[:, None] * turn_rate[None, :]
    cosine = jnp.cos(angles)
    sine = jnp.sin(angles)
    growth = jnp.exp(offsets[None, :, None] * decay_rate[None, None, :] - keep_cum)
    blk_re = drive_re.reshape(block_count, block_len, num_cols)
    blk_im = drive_im.reshape(block_count, block_len, num_cols)
    pre_re = growth * (blk_re * cosine + blk_im * sine)
    pre_im = growth * (blk_im * cosine - blk_re * sine)
    lower_ones = (offsets[:, None] >= offsets[None, :]).astype(jnp.float32)
    summed = jnp.einsum(
        "ji,abik->abjk", lower_ones, jnp.stack([pre_re, pre_im]), precision=lax.Precision.HIGHEST
    )
    shrink = jnp.exp(keep_cum - offsets[None, :, None] * decay_rate[None, None, :])
    state_re = shrink * (summed[0] * cosine - summed[1] * sine)
    state_im = shrink * (summed[0] * sine + summed[1] * cosine)
    step_mag = jnp.exp(keep_cum[:, -1] - block_len * decay_rate[None, :])
    step_re = step_mag * jnp.cos(block_len * turn_rate)[None, :]
    step_im = step_mag * jnp.sin(block_len * turn_rate)[None, :]

    def advance(carried, inputs):
        carry_re, carry_im = carried
        mult_re, mult_im, end_re, end_im = inputs
        next_re = mult_re * carry_re - mult_im * carry_im + end_re
        next_im = mult_re * carry_im + mult_im * carry_re + end_im
        return ((next_re, next_im), (carry_re, carry_im))

    zeros_col = jnp.zeros((num_cols,), jnp.float32)
    enter_re, enter_im = lax.scan(
        advance, (zeros_col, zeros_col), (step_re, step_im, state_re[:, -1], state_im[:, -1])
    )[1]
    ahead = offsets + 1.0
    lift = jnp.exp(keep_cum - ahead[None, :, None] * decay_rate[None, None, :])
    lift_re = lift * jnp.cos(ahead[:, None] * turn_rate[None, :])
    lift_im = lift * jnp.sin(ahead[:, None] * turn_rate[None, :])
    state_re = state_re + lift_re * enter_re[:, None] - lift_im * enter_im[:, None]
    state_im = state_im + lift_re * enter_im[:, None] + lift_im * enter_re[:, None]
    return (state_re.reshape(seq_len, num_cols), state_im.reshape(seq_len, num_cols))


def carry_combine(earlier, later):
    early_re, early_im, early_sre, early_sim = earlier
    late_re, late_im, late_sre, late_sim = later
    joined_re = early_re * late_re - early_im * late_im
    joined_im = early_re * late_im + early_im * late_re
    joined_sre = late_re * early_sre - late_im * early_sim + late_sre
    joined_sim = late_re * early_sim + late_im * early_sre + late_sim
    return (joined_re, joined_im, joined_sre, joined_sim)


def per_device(
    tokens,
    conv_taps,
    log_rate,
    rotation,
    in_proj,
    out_proj,
    skip_gain,
    norm_gain,
    retention,
    cotangent,
):
    seq_len, local_width = tokens.shape
    tap_count = conv_taps.shape[0]
    local_heads, head_width, double_state = in_proj.shape
    state_size = double_state // 2
    num_cols = local_heads * state_size
    lead_rows = from_behind(tokens[seq_len - (tap_count - 1) :], "seq", 1)
    padded = jnp.concatenate([lead_rows, tokens], axis=0).astype(jnp.float32)
    conv_sum = conv_taps[0][None, :] * padded[tap_count - 1 :]
    for offset in range(1, tap_count):
        conv_sum = (
            conv_sum
            + conv_taps[offset][None, :]
            * padded[tap_count - 1 - offset : tap_count - 1 - offset + seq_len]
        )
    mixed_in = conv_sum.astype(jnp.bfloat16)
    by_head = mixed_in.reshape(seq_len, local_heads, head_width)
    projected = jnp.einsum("thc,hck->thk", by_head, in_proj, preferred_element_type=jnp.float32)
    in_scale = jnp.sqrt(-jnp.expm1(-2.0 * log_rate))
    drive_re = projected[:, :, :state_size].reshape(seq_len, num_cols) * in_scale
    drive_im = projected[:, :, state_size:].reshape(seq_len, num_cols) * in_scale
    log_keep = jnp.log(retention)
    state_re, state_im = linear_run(drive_re, drive_im, log_rate, rotation, log_keep)
    keep_total = jnp.sum(log_keep)
    total_mag = jnp.exp(keep_total - seq_len * log_rate)
    total_re = total_mag * jnp.cos(seq_len * rotation)
    total_im = total_mag * jnp.sin(seq_len * rotation)
    unit_ones = jnp.ones((num_cols,), jnp.float32)
    zeros_col = jnp.zeros((num_cols,), jnp.float32)
    chained = carried_in(
        (total_re, total_im, state_re[-1], state_im[-1]),
        "seq",
        carry_combine,
        (unit_ones, zeros_col, zeros_col, zeros_col),
        False,
    )
    enter_re, enter_im = (chained[2], chained[3])
    positions = jnp.arange(seq_len, dtype=jnp.float32)
    ahead = positions + 1.0
    lift = jnp.exp(jnp.cumsum(log_keep)[:, None] - ahead[:, None] * log_rate[None, :])
    lift_re = lift * jnp.cos(ahead[:, None] * rotation[None, :])
    lift_im = lift * jnp.sin(ahead[:, None] * rotation[None, :])
    state_re = state_re + lift_re * enter_re[None, :] - lift_im * enter_im[None, :]
    state_im = state_im + lift_re * enter_im[None, :] + lift_im * enter_re[None, :]
    state_bf = jnp.concatenate(
        [
            state_re.reshape(seq_len, local_heads, state_size),
            state_im.reshape(seq_len, local_heads, state_size),
        ],
        axis=2,
    ).astype(jnp.bfloat16)
    mixed = jnp.einsum(
        "thk,hck->thc", state_bf, out_proj, preferred_element_type=jnp.float32
    ).reshape(seq_len, local_width)
    mixed = mixed + skip_gain * mixed_in.astype(jnp.float32)
    squares = jnp.sum(mixed * mixed, axis=1)
    scaled = cotangent.astype(jnp.float32) * norm_gain
    dots = jnp.sum(scaled * mixed, axis=1)
    squares = lax.psum(squares, "chan")
    model_width = local_width * lax.axis_size("chan")
    inverse = lax.rsqrt(squares / model_width + 1e-06)
    normed = (mixed * inverse[:, None] * norm_gain).astype(jnp.bfloat16)
    dots = lax.psum(dots, "chan")
    mixed_grad = inverse[:, None] * (
        scaled - mixed * (inverse * inverse * dots / model_width)[:, None]
    )
    grad_bf = mixed_grad.astype(jnp.bfloat16).reshape(seq_len, local_heads, head_width)
    state_grad = jnp.einsum("thc,hck->thk", grad_bf, out_proj, preferred_element_type=jnp.float32)
    out_grad = jnp.einsum("thc,thk->hck", grad_bf, state_bf, preferred_element_type=jnp.float32)
    back_keep = jnp.concatenate([jnp.zeros((1,), jnp.float32), log_keep[::-1][:-1]])
    grad_re = state_grad[:, :, :state_size].reshape(seq_len, num_cols)[::-1]
    grad_im = state_grad[:, :, state_size:].reshape(seq_len, num_cols)[::-1]
    adj_re, adj_im = linear_run(grad_re, grad_im, log_rate, -rotation, back_keep)
    first_mag = jnp.exp(log_keep[0] - log_rate)
    cos_turn = jnp.cos(rotation)
    sin_turn = jnp.sin(rotation)
    first_re = first_mag * (cos_turn * adj_re[-1] + sin_turn * adj_im[-1])
    first_im = first_mag * (cos_turn * adj_im[-1] - sin_turn * adj_re[-1])
    back_chained = carried_in(
        (total_re, -total_im, first_re, first_im),
        "seq",
        carry_combine,
        (unit_ones, zeros_col, zeros_col, zeros_col),
        True,
    )
    later_re, later_im = (back_chained[2], back_chained[3])
    back_lift = jnp.exp(jnp.cumsum(back_keep)[:, None] - positions[:, None] * log_rate[None, :])
    back_re = back_lift * jnp.cos(positions[:, None] * rotation[None, :])
    back_im = -back_lift * jnp.sin(positions[:, None] * rotation[None, :])
    adj_re = adj_re + back_re * later_re[None, :] - back_im * later_im[None, :]
    adj_im = adj_im + back_re * later_im[None, :] + back_im * later_re[None, :]
    adj_re = adj_re[::-1]
    adj_im = adj_im[::-1]
    drive_grad = jnp.concatenate(
        [
            (in_scale * adj_re).reshape(seq_len, local_heads, state_size),
            (in_scale * adj_im).reshape(seq_len, local_heads, state_size),
        ],
        axis=2,
    ).astype(jnp.bfloat16)
    in_grad = jnp.einsum("thc,thk->hck", by_head, drive_grad, preferred_element_type=jnp.float32)
    input_grad = jnp.einsum(
        "thk,hck->thc", drive_grad, in_proj, preferred_element_type=jnp.float32
    ).reshape(seq_len, local_width)
    input_grad = input_grad + skip_gain * mixed_grad
    trail_rows = from_behind(input_grad[: tap_count - 1], "seq", -1)
    tail = jnp.concatenate([input_grad, trail_rows], axis=0)
    tokens_grad = conv_taps[0][None, :] * tail[:seq_len]
    for offset in range(1, tap_count):
        tokens_grad = tokens_grad + conv_taps[offset][None, :] * tail[offset : offset + seq_len]
    taps_grad = jnp.stack(
        [
            jnp.sum(
                input_grad * padded[tap_count - 1 - offset : tap_count - 1 - offset + seq_len],
                axis=0,
            )
            for offset in range(tap_count)
        ]
    )
    in_grad, out_grad, taps_grad = lax.psum((in_grad, out_grad, taps_grad), "seq")
    return (normed, tokens_grad.astype(jnp.bfloat16), in_grad, out_grad, taps_grad)


def solution(mesh):
    in_specs = (
        P("seq", "chan"),
        P(None, "chan"),
        P("chan"),
        P("chan"),
        P("chan", None, None),
        P("chan", None, None),
        P("chan"),
        P("chan"),
        P("seq"),
        P("seq", "chan"),
    )
    out_specs = (
        P("seq", "chan"),
        P("seq", "chan"),
        P("chan", None, None),
        P("chan", None, None),
        P(None, "chan"),
    )
    return jax.shard_map(
        per_device, mesh=mesh, in_specs=in_specs, out_specs=out_specs, check_vma=False
    )
```

```python
import jax
import jax.numpy as jnp
from jax import lax
from jax.sharding import Mesh, PartitionSpec as P

SEQ = ("z", "y")


def from_behind(value, axis, by):
    length = lax.axis_size(axis)
    pairs = [(i, i + by) for i in range(length) if 0 <= i + by < length]
    return lax.ppermute(value, axis, pairs)


def carried_in(part, axis, combine, identity, reverse):
    count = lax.axis_size(axis)
    place = lax.axis_index(axis)
    ahead = count - 1 - place if reverse else place
    step = -1 if reverse else 1
    packed = jnp.stack(part)
    unit = jnp.stack([jnp.zeros_like(a) + jnp.asarray(e, a.dtype) for a, e in zip(part, identity)])
    state = jnp.where(ahead >= 1, from_behind(packed, axis, step), unit)
    reach = 1
    while reach < count:
        earlier = from_behind(state, axis, step * reach)
        joined = jnp.stack(combine(tuple(earlier), tuple(state)))
        state = jnp.where(ahead >= reach, joined, state)
        reach *= 2
    return tuple(state)


def linear_run(drive_re, drive_im, decay_rate, turn_rate, log_keep):
    seq_len, num_cols = drive_re.shape
    block_len = min(64, seq_len)
    block_count = seq_len // block_len
    offsets = jnp.arange(block_len, dtype=jnp.float32)
    keep_cum = jnp.cumsum(log_keep.reshape(block_count, block_len), axis=1)[:, :, None]
    angles = offsets[:, None] * turn_rate[None, :]
    cosine = jnp.cos(angles)
    sine = jnp.sin(angles)
    growth = jnp.exp(offsets[None, :, None] * decay_rate[None, None, :] - keep_cum)
    blk_re = drive_re.reshape(block_count, block_len, num_cols)
    blk_im = drive_im.reshape(block_count, block_len, num_cols)
    pre_re = growth * (blk_re * cosine + blk_im * sine)
    pre_im = growth * (blk_im * cosine - blk_re * sine)
    lower_ones = (offsets[:, None] >= offsets[None, :]).astype(jnp.float32)
    summed = jnp.einsum(
        "ji,abik->abjk", lower_ones, jnp.stack([pre_re, pre_im]), precision=lax.Precision.HIGHEST
    )
    shrink = jnp.exp(keep_cum - offsets[None, :, None] * decay_rate[None, None, :])
    state_re = shrink * (summed[0] * cosine - summed[1] * sine)
    state_im = shrink * (summed[0] * sine + summed[1] * cosine)
    step_mag = jnp.exp(keep_cum[:, -1] - block_len * decay_rate[None, :])
    step_re = step_mag * jnp.cos(block_len * turn_rate)[None, :]
    step_im = step_mag * jnp.sin(block_len * turn_rate)[None, :]

    def advance(carried, inputs):
        carry_re, carry_im = carried
        mult_re, mult_im, end_re, end_im = inputs
        next_re = mult_re * carry_re - mult_im * carry_im + end_re
        next_im = mult_re * carry_im + mult_im * carry_re + end_im
        return ((next_re, next_im), (carry_re, carry_im))

    zeros_col = jnp.zeros((num_cols,), jnp.float32)
    enter_re, enter_im = lax.scan(
        advance, (zeros_col, zeros_col), (step_re, step_im, state_re[:, -1], state_im[:, -1])
    )[1]
    ahead = offsets + 1.0
    lift = jnp.exp(keep_cum - ahead[None, :, None] * decay_rate[None, None, :])
    lift_re = lift * jnp.cos(ahead[:, None] * turn_rate[None, :])
    lift_im = lift * jnp.sin(ahead[:, None] * turn_rate[None, :])
    state_re = state_re + lift_re * enter_re[:, None] - lift_im * enter_im[:, None]
    state_im = state_im + lift_re * enter_im[:, None] + lift_im * enter_re[:, None]
    return (state_re.reshape(seq_len, num_cols), state_im.reshape(seq_len, num_cols))


def carry_combine(earlier, later):
    early_re, early_im, early_sre, early_sim = earlier
    late_re, late_im, late_sre, late_sim = later
    joined_re = early_re * late_re - early_im * late_im
    joined_im = early_re * late_im + early_im * late_re
    joined_sre = late_re * early_sre - late_im * early_sim + late_sre
    joined_sim = late_re * early_sim + late_im * early_sre + late_sim
    return (joined_re, joined_im, joined_sre, joined_sim)


def per_device(
    tokens,
    conv_taps,
    log_rate,
    rotation,
    in_proj,
    out_proj,
    skip_gain,
    norm_gain,
    retention,
    cotangent,
):
    seq_len, local_width = tokens.shape
    tap_count = conv_taps.shape[0]
    local_heads, head_width, double_state = in_proj.shape
    state_size = double_state // 2
    num_cols = local_heads * state_size
    lead_rows = from_behind(tokens[seq_len - (tap_count - 1) :], SEQ, 1)
    padded = jnp.concatenate([lead_rows, tokens], axis=0).astype(jnp.float32)
    conv_sum = conv_taps[0][None, :] * padded[tap_count - 1 :]
    for offset in range(1, tap_count):
        conv_sum = (
            conv_sum
            + conv_taps[offset][None, :]
            * padded[tap_count - 1 - offset : tap_count - 1 - offset + seq_len]
        )
    mixed_in = conv_sum.astype(jnp.bfloat16)
    by_head = mixed_in.reshape(seq_len, local_heads, head_width)
    projected = jnp.einsum("thc,hck->thk", by_head, in_proj, preferred_element_type=jnp.float32)
    in_scale = jnp.sqrt(-jnp.expm1(-2.0 * log_rate))
    drive_re = projected[:, :, :state_size].reshape(seq_len, num_cols) * in_scale
    drive_im = projected[:, :, state_size:].reshape(seq_len, num_cols) * in_scale
    log_keep = jnp.log(retention)
    state_re, state_im = linear_run(drive_re, drive_im, log_rate, rotation, log_keep)
    keep_total = jnp.sum(log_keep)
    total_mag = jnp.exp(keep_total - seq_len * log_rate)
    total_re = total_mag * jnp.cos(seq_len * rotation)
    total_im = total_mag * jnp.sin(seq_len * rotation)
    unit_ones = jnp.ones((num_cols,), jnp.float32)
    zeros_col = jnp.zeros((num_cols,), jnp.float32)
    chained = carried_in(
        (total_re, total_im, state_re[-1], state_im[-1]),
        SEQ,
        carry_combine,
        (unit_ones, zeros_col, zeros_col, zeros_col),
        False,
    )
    enter_re, enter_im = (chained[2], chained[3])
    positions = jnp.arange(seq_len, dtype=jnp.float32)
    ahead = positions + 1.0
    lift = jnp.exp(jnp.cumsum(log_keep)[:, None] - ahead[:, None] * log_rate[None, :])
    lift_re = lift * jnp.cos(ahead[:, None] * rotation[None, :])
    lift_im = lift * jnp.sin(ahead[:, None] * rotation[None, :])
    state_re = state_re + lift_re * enter_re[None, :] - lift_im * enter_im[None, :]
    state_im = state_im + lift_re * enter_im[None, :] + lift_im * enter_re[None, :]
    state_bf = jnp.concatenate(
        [
            state_re.reshape(seq_len, local_heads, state_size),
            state_im.reshape(seq_len, local_heads, state_size),
        ],
        axis=2,
    ).astype(jnp.bfloat16)
    mixed = jnp.einsum(
        "thk,hck->thc", state_bf, out_proj, preferred_element_type=jnp.float32
    ).reshape(seq_len, local_width)
    mixed = mixed + skip_gain * mixed_in.astype(jnp.float32)
    squares = jnp.sum(mixed * mixed, axis=1)
    scaled = cotangent.astype(jnp.float32) * norm_gain
    dots = jnp.sum(scaled * mixed, axis=1)
    squares = lax.psum(squares, "chan")
    model_width = local_width * lax.axis_size("chan")
    inverse = lax.rsqrt(squares / model_width + 1e-06)
    normed = (mixed * inverse[:, None] * norm_gain).astype(jnp.bfloat16)
    dots = lax.psum(dots, "chan")
    mixed_grad = inverse[:, None] * (
        scaled - mixed * (inverse * inverse * dots / model_width)[:, None]
    )
    grad_bf = mixed_grad.astype(jnp.bfloat16).reshape(seq_len, local_heads, head_width)
    state_grad = jnp.einsum("thc,hck->thk", grad_bf, out_proj, preferred_element_type=jnp.float32)
    out_grad = jnp.einsum("thc,thk->hck", grad_bf, state_bf, preferred_element_type=jnp.float32)
    out_grad = lax.psum(lax.psum(out_grad, "y"), "z")
    back_keep = jnp.concatenate([jnp.zeros((1,), jnp.float32), log_keep[::-1][:-1]])
    grad_re = state_grad[:, :, :state_size].reshape(seq_len, num_cols)[::-1]
    grad_im = state_grad[:, :, state_size:].reshape(seq_len, num_cols)[::-1]
    adj_re, adj_im = linear_run(grad_re, grad_im, log_rate, -rotation, back_keep)
    first_mag = jnp.exp(log_keep[0] - log_rate)
    cos_turn = jnp.cos(rotation)
    sin_turn = jnp.sin(rotation)
    first_re = first_mag * (cos_turn * adj_re[-1] + sin_turn * adj_im[-1])
    first_im = first_mag * (cos_turn * adj_im[-1] - sin_turn * adj_re[-1])
    back_chained = carried_in(
        (total_re, -total_im, first_re, first_im),
        SEQ,
        carry_combine,
        (unit_ones, zeros_col, zeros_col, zeros_col),
        True,
    )
    later_re, later_im = (back_chained[2], back_chained[3])
    back_lift = jnp.exp(jnp.cumsum(back_keep)[:, None] - positions[:, None] * log_rate[None, :])
    back_re = back_lift * jnp.cos(positions[:, None] * rotation[None, :])
    back_im = -back_lift * jnp.sin(positions[:, None] * rotation[None, :])
    adj_re = adj_re + back_re * later_re[None, :] - back_im * later_im[None, :]
    adj_im = adj_im + back_re * later_im[None, :] + back_im * later_re[None, :]
    adj_re = adj_re[::-1]
    adj_im = adj_im[::-1]
    drive_grad = jnp.concatenate(
        [
            (in_scale * adj_re).reshape(seq_len, local_heads, state_size),
            (in_scale * adj_im).reshape(seq_len, local_heads, state_size),
        ],
        axis=2,
    ).astype(jnp.bfloat16)
    in_grad = jnp.einsum("thc,thk->hck", by_head, drive_grad, preferred_element_type=jnp.float32)
    input_grad = jnp.einsum(
        "thk,hck->thc", drive_grad, in_proj, preferred_element_type=jnp.float32
    ).reshape(seq_len, local_width)
    input_grad = input_grad + skip_gain * mixed_grad
    trail_rows = from_behind(input_grad[: tap_count - 1], SEQ, -1)
    tail = jnp.concatenate([input_grad, trail_rows], axis=0)
    tokens_grad = conv_taps[0][None, :] * tail[:seq_len]
    for offset in range(1, tap_count):
        tokens_grad = tokens_grad + conv_taps[offset][None, :] * tail[offset : offset + seq_len]
    taps_grad = jnp.stack(
        [
            jnp.sum(
                input_grad * padded[tap_count - 1 - offset : tap_count - 1 - offset + seq_len],
                axis=0,
            )
            for offset in range(tap_count)
        ]
    )
    packed = jnp.concatenate([in_grad.reshape(-1), taps_grad.reshape(-1)])
    packed = lax.psum(lax.psum(packed, "y"), "z")
    in_grad = packed[: in_grad.size].reshape(in_grad.shape)
    taps_grad = packed[in_grad.size :].reshape(taps_grad.shape)
    return (normed, tokens_grad.astype(jnp.bfloat16), in_grad, out_grad, taps_grad)


def solution(mesh):
    seq_count, chan_count = mesh.devices.shape
    inner = 1
    while inner * inner < seq_count:
        inner *= 2
    devices = mesh.devices.reshape(seq_count // inner, inner, chan_count)
    mesh = Mesh(devices, SEQ + ("chan",))
    in_specs = (
        P(SEQ, "chan"),
        P(None, "chan"),
        P("chan"),
        P("chan"),
        P("chan", None, None),
        P("chan", None, None),
        P("chan"),
        P("chan"),
        P(SEQ),
        P(SEQ, "chan"),
    )
    out_specs = (
        P(SEQ, "chan"),
        P(SEQ, "chan"),
        P("chan", None, None),
        P("chan", None, None),
        P(None, "chan"),
    )
    return jax.shard_map(
        per_device, mesh=mesh, in_specs=in_specs, out_specs=out_specs, check_vma=False
    )
```

```python
import jax
import jax.numpy as jnp
from jax import lax
from jax.sharding import Mesh, PartitionSpec as P

SEQ = ("z", "y")


def from_behind(value, axis, by):
    length = lax.axis_size(axis)
    pairs = [(i, i + by) for i in range(length) if 0 <= i + by < length]
    return lax.ppermute(value, axis, pairs)


def carried_in(part, axis, combine, identity, reverse):
    count = lax.axis_size(axis)
    place = lax.axis_index(axis)
    ahead = count - 1 - place if reverse else place
    step = -1 if reverse else 1
    packed = jnp.stack(part)
    unit = jnp.stack([jnp.zeros_like(a) + jnp.asarray(e, a.dtype) for a, e in zip(part, identity)])
    state = jnp.where(ahead >= 1, from_behind(packed, axis, step), unit)
    reach = 1
    while reach < count:
        earlier = from_behind(state, axis, step * reach)
        joined = jnp.stack(combine(tuple(earlier), tuple(state)))
        state = jnp.where(ahead >= reach, joined, state)
        reach *= 2
    return tuple(state)


def tree_sum(value, axis):
    count = lax.axis_size(axis)
    place = lax.axis_index(axis)
    flat = value.reshape(-1)
    width = -(-flat.size // count)
    block = jnp.pad(flat, (0, width * count - flat.size)).reshape(count, width)
    bits = []
    span = 1
    while span < count:
        bits.append(span)
        span *= 2
    order = bits[0::3] + bits[1::3] + bits[2::3]
    for span in order:
        upper = (place // span) % 2 == 1
        half = block.shape[0] // 2
        low, high = block[:half], block[half:]
        pairs = [(i, i ^ span) for i in range(count)]
        sent = lax.ppermute(jnp.where(upper, low, high), axis, pairs)
        block = jnp.where(upper, high, low) + sent
    for span in order[::-1]:
        upper = (place // span) % 2 == 1
        pairs = [(i, i ^ span) for i in range(count)]
        other = lax.ppermute(block, axis, pairs)
        block = jnp.where(upper, jnp.concatenate([other, block]), jnp.concatenate([block, other]))
    return block.reshape(-1)[: flat.size].reshape(value.shape)


def linear_run(drive_re, drive_im, decay_rate, turn_rate, log_keep):
    seq_len, num_cols = drive_re.shape
    block_len = min(64, seq_len)
    block_count = seq_len // block_len
    offsets = jnp.arange(block_len, dtype=jnp.float32)
    keep_cum = jnp.cumsum(log_keep.reshape(block_count, block_len), axis=1)[:, :, None]
    angles = offsets[:, None] * turn_rate[None, :]
    cosine = jnp.cos(angles)
    sine = jnp.sin(angles)
    growth = jnp.exp(offsets[None, :, None] * decay_rate[None, None, :] - keep_cum)
    blk_re = drive_re.reshape(block_count, block_len, num_cols)
    blk_im = drive_im.reshape(block_count, block_len, num_cols)
    pre_re = growth * (blk_re * cosine + blk_im * sine)
    pre_im = growth * (blk_im * cosine - blk_re * sine)
    lower_ones = (offsets[:, None] >= offsets[None, :]).astype(jnp.float32)
    summed = jnp.einsum(
        "ji,abik->abjk", lower_ones, jnp.stack([pre_re, pre_im]), precision=lax.Precision.HIGHEST
    )
    shrink = jnp.exp(keep_cum - offsets[None, :, None] * decay_rate[None, None, :])
    state_re = shrink * (summed[0] * cosine - summed[1] * sine)
    state_im = shrink * (summed[0] * sine + summed[1] * cosine)
    step_mag = jnp.exp(keep_cum[:, -1] - block_len * decay_rate[None, :])
    step_re = step_mag * jnp.cos(block_len * turn_rate)[None, :]
    step_im = step_mag * jnp.sin(block_len * turn_rate)[None, :]

    def advance(carried, inputs):
        carry_re, carry_im = carried
        mult_re, mult_im, end_re, end_im = inputs
        next_re = mult_re * carry_re - mult_im * carry_im + end_re
        next_im = mult_re * carry_im + mult_im * carry_re + end_im
        return ((next_re, next_im), (carry_re, carry_im))

    zeros_col = jnp.zeros((num_cols,), jnp.float32)
    enter_re, enter_im = lax.scan(
        advance, (zeros_col, zeros_col), (step_re, step_im, state_re[:, -1], state_im[:, -1])
    )[1]
    ahead = offsets + 1.0
    lift = jnp.exp(keep_cum - ahead[None, :, None] * decay_rate[None, None, :])
    lift_re = lift * jnp.cos(ahead[:, None] * turn_rate[None, :])
    lift_im = lift * jnp.sin(ahead[:, None] * turn_rate[None, :])
    state_re = state_re + lift_re * enter_re[:, None] - lift_im * enter_im[:, None]
    state_im = state_im + lift_re * enter_im[:, None] + lift_im * enter_re[:, None]
    return (state_re.reshape(seq_len, num_cols), state_im.reshape(seq_len, num_cols))


def carry_combine(earlier, later):
    early_re, early_im, early_sre, early_sim = earlier
    late_re, late_im, late_sre, late_sim = later
    joined_re = early_re * late_re - early_im * late_im
    joined_im = early_re * late_im + early_im * late_re
    joined_sre = late_re * early_sre - late_im * early_sim + late_sre
    joined_sim = late_re * early_sim + late_im * early_sre + late_sim
    return (joined_re, joined_im, joined_sre, joined_sim)


def per_device(
    tokens,
    conv_taps,
    log_rate,
    rotation,
    in_proj,
    out_proj,
    skip_gain,
    norm_gain,
    retention,
    cotangent,
):
    seq_len, local_width = tokens.shape
    tap_count = conv_taps.shape[0]
    local_heads, head_width, double_state = in_proj.shape
    state_size = double_state // 2
    num_cols = local_heads * state_size
    lead_rows = from_behind(tokens[seq_len - (tap_count - 1) :], SEQ, 1)
    padded = jnp.concatenate([lead_rows, tokens], axis=0).astype(jnp.float32)
    conv_sum = conv_taps[0][None, :] * padded[tap_count - 1 :]
    for offset in range(1, tap_count):
        conv_sum = (
            conv_sum
            + conv_taps[offset][None, :]
            * padded[tap_count - 1 - offset : tap_count - 1 - offset + seq_len]
        )
    mixed_in = conv_sum.astype(jnp.bfloat16)
    by_head = mixed_in.reshape(seq_len, local_heads, head_width)
    projected = jnp.einsum("thc,hck->thk", by_head, in_proj, preferred_element_type=jnp.float32)
    in_scale = jnp.sqrt(-jnp.expm1(-2.0 * log_rate))
    drive_re = projected[:, :, :state_size].reshape(seq_len, num_cols) * in_scale
    drive_im = projected[:, :, state_size:].reshape(seq_len, num_cols) * in_scale
    log_keep = jnp.log(retention)
    state_re, state_im = linear_run(drive_re, drive_im, log_rate, rotation, log_keep)
    keep_total = jnp.sum(log_keep)
    total_mag = jnp.exp(keep_total - seq_len * log_rate)
    total_re = total_mag * jnp.cos(seq_len * rotation)
    total_im = total_mag * jnp.sin(seq_len * rotation)
    unit_ones = jnp.ones((num_cols,), jnp.float32)
    zeros_col = jnp.zeros((num_cols,), jnp.float32)
    chained = carried_in(
        (total_re, total_im, state_re[-1], state_im[-1]),
        SEQ,
        carry_combine,
        (unit_ones, zeros_col, zeros_col, zeros_col),
        False,
    )
    enter_re, enter_im = (chained[2], chained[3])
    positions = jnp.arange(seq_len, dtype=jnp.float32)
    ahead = positions + 1.0
    lift = jnp.exp(jnp.cumsum(log_keep)[:, None] - ahead[:, None] * log_rate[None, :])
    lift_re = lift * jnp.cos(ahead[:, None] * rotation[None, :])
    lift_im = lift * jnp.sin(ahead[:, None] * rotation[None, :])
    state_re = state_re + lift_re * enter_re[None, :] - lift_im * enter_im[None, :]
    state_im = state_im + lift_re * enter_im[None, :] + lift_im * enter_re[None, :]
    state_bf = jnp.concatenate(
        [
            state_re.reshape(seq_len, local_heads, state_size),
            state_im.reshape(seq_len, local_heads, state_size),
        ],
        axis=2,
    ).astype(jnp.bfloat16)
    mixed = jnp.einsum(
        "thk,hck->thc", state_bf, out_proj, preferred_element_type=jnp.float32
    ).reshape(seq_len, local_width)
    mixed = mixed + skip_gain * mixed_in.astype(jnp.float32)
    squares = jnp.sum(mixed * mixed, axis=1)
    scaled = cotangent.astype(jnp.float32) * norm_gain
    dots = jnp.sum(scaled * mixed, axis=1)
    squares = lax.psum(squares, "chan")
    model_width = local_width * lax.axis_size("chan")
    inverse = lax.rsqrt(squares / model_width + 1e-06)
    normed = (mixed * inverse[:, None] * norm_gain).astype(jnp.bfloat16)
    dots = lax.psum(dots, "chan")
    mixed_grad = inverse[:, None] * (
        scaled - mixed * (inverse * inverse * dots / model_width)[:, None]
    )
    grad_bf = mixed_grad.astype(jnp.bfloat16).reshape(seq_len, local_heads, head_width)
    state_grad = jnp.einsum("thc,hck->thk", grad_bf, out_proj, preferred_element_type=jnp.float32)
    out_grad = jnp.einsum("thc,thk->hck", grad_bf, state_bf, preferred_element_type=jnp.float32)
    out_grad = tree_sum(out_grad, SEQ)
    back_keep = jnp.concatenate([jnp.zeros((1,), jnp.float32), log_keep[::-1][:-1]])
    grad_re = state_grad[:, :, :state_size].reshape(seq_len, num_cols)[::-1]
    grad_im = state_grad[:, :, state_size:].reshape(seq_len, num_cols)[::-1]
    adj_re, adj_im = linear_run(grad_re, grad_im, log_rate, -rotation, back_keep)
    first_mag = jnp.exp(log_keep[0] - log_rate)
    cos_turn = jnp.cos(rotation)
    sin_turn = jnp.sin(rotation)
    first_re = first_mag * (cos_turn * adj_re[-1] + sin_turn * adj_im[-1])
    first_im = first_mag * (cos_turn * adj_im[-1] - sin_turn * adj_re[-1])
    back_chained = carried_in(
        (total_re, -total_im, first_re, first_im),
        SEQ,
        carry_combine,
        (unit_ones, zeros_col, zeros_col, zeros_col),
        True,
    )
    later_re, later_im = (back_chained[2], back_chained[3])
    back_lift = jnp.exp(jnp.cumsum(back_keep)[:, None] - positions[:, None] * log_rate[None, :])
    back_re = back_lift * jnp.cos(positions[:, None] * rotation[None, :])
    back_im = -back_lift * jnp.sin(positions[:, None] * rotation[None, :])
    adj_re = adj_re + back_re * later_re[None, :] - back_im * later_im[None, :]
    adj_im = adj_im + back_re * later_im[None, :] + back_im * later_re[None, :]
    adj_re = adj_re[::-1]
    adj_im = adj_im[::-1]
    drive_grad = jnp.concatenate(
        [
            (in_scale * adj_re).reshape(seq_len, local_heads, state_size),
            (in_scale * adj_im).reshape(seq_len, local_heads, state_size),
        ],
        axis=2,
    ).astype(jnp.bfloat16)
    in_grad = jnp.einsum("thc,thk->hck", by_head, drive_grad, preferred_element_type=jnp.float32)
    input_grad = jnp.einsum(
        "thk,hck->thc", drive_grad, in_proj, preferred_element_type=jnp.float32
    ).reshape(seq_len, local_width)
    input_grad = input_grad + skip_gain * mixed_grad
    trail_rows = from_behind(input_grad[: tap_count - 1], SEQ, -1)
    tail = jnp.concatenate([input_grad, trail_rows], axis=0)
    tokens_grad = conv_taps[0][None, :] * tail[:seq_len]
    for offset in range(1, tap_count):
        tokens_grad = tokens_grad + conv_taps[offset][None, :] * tail[offset : offset + seq_len]
    taps_grad = jnp.stack(
        [
            jnp.sum(
                input_grad * padded[tap_count - 1 - offset : tap_count - 1 - offset + seq_len],
                axis=0,
            )
            for offset in range(tap_count)
        ]
    )
    packed = jnp.concatenate([in_grad.reshape(-1), taps_grad.reshape(-1)])
    packed = tree_sum(packed, SEQ)
    in_grad = packed[: in_grad.size].reshape(in_grad.shape)
    taps_grad = packed[in_grad.size :].reshape(taps_grad.shape)
    return (normed, tokens_grad.astype(jnp.bfloat16), in_grad, out_grad, taps_grad)


def solution(mesh):
    seq_count, chan_count = mesh.devices.shape
    inner = 1
    while inner * inner < seq_count:
        inner *= 2
    devices = mesh.devices.reshape(seq_count // inner, inner, chan_count)
    mesh = Mesh(devices, SEQ + ("chan",))
    in_specs = (
        P(SEQ, "chan"),
        P(None, "chan"),
        P("chan"),
        P("chan"),
        P("chan", None, None),
        P("chan", None, None),
        P("chan"),
        P("chan"),
        P(SEQ),
        P(SEQ, "chan"),
    )
    out_specs = (
        P(SEQ, "chan"),
        P(SEQ, "chan"),
        P("chan", None, None),
        P("chan", None, None),
        P(None, "chan"),
    )
    return jax.shard_map(
        per_device, mesh=mesh, in_specs=in_specs, out_specs=out_specs, check_vma=False
    )
```

```python
import jax
import jax.numpy as jnp
from jax import lax
from jax.sharding import Mesh, PartitionSpec as P

SEQ = ("z", "y")


def from_behind(value, axis, by):
    length = lax.axis_size(axis)
    pairs = [(i, i + by) for i in range(length) if 0 <= i + by < length]
    return lax.ppermute(value, axis, pairs)


def fold(stack, where_at, combine, unit):
    total = unit
    prefix = unit
    for j in range(stack.shape[0]):
        prefix = jnp.where(j == where_at, total, prefix)
        total = jnp.stack(combine(tuple(total), tuple(stack[j])))
    return prefix, total


def carried_in(part, axis, combine, identity, reverse):
    outer, inner = axis
    packed = jnp.stack(part)
    unit = jnp.stack([jnp.zeros_like(a) + jnp.asarray(e, a.dtype) for a, e in zip(part, identity)])
    row_place = lax.axis_index(inner)
    col_place = lax.axis_index(outer)
    row = lax.all_gather(packed, inner)
    if reverse:
        row = row[::-1]
        row_place = lax.axis_size(inner) - 1 - row_place
        col_place = lax.axis_size(outer) - 1 - col_place
    within, row_total = fold(row, row_place, combine, unit)
    rows = lax.all_gather(row_total, outer)
    if reverse:
        rows = rows[::-1]
    before, _ = fold(rows, col_place, combine, unit)
    return combine(tuple(before), tuple(within))


def tree_sum(value, axis):
    count = lax.axis_size(axis)
    place = lax.axis_index(axis)
    flat = value.reshape(-1)
    width = -(-flat.size // count)
    block = jnp.pad(flat, (0, width * count - flat.size)).reshape(count, width)
    bits = []
    span = 1
    while span < count:
        bits.append(span)
        span *= 2
    order = bits[0::3] + bits[1::3] + bits[2::3]
    for span in order:
        upper = (place // span) % 2 == 1
        half = block.shape[0] // 2
        low, high = block[:half], block[half:]
        pairs = [(i, i ^ span) for i in range(count)]
        sent = lax.ppermute(jnp.where(upper, low, high), axis, pairs)
        block = jnp.where(upper, high, low) + sent
    for span in order[::-1]:
        upper = (place // span) % 2 == 1
        pairs = [(i, i ^ span) for i in range(count)]
        other = lax.ppermute(block, axis, pairs)
        block = jnp.where(upper, jnp.concatenate([other, block]), jnp.concatenate([block, other]))
    return block.reshape(-1)[: flat.size].reshape(value.shape)


def linear_run(drive_re, drive_im, decay_rate, turn_rate, log_keep):
    seq_len, num_cols = drive_re.shape
    block_len = min(64, seq_len)
    block_count = seq_len // block_len
    offsets = jnp.arange(block_len, dtype=jnp.float32)
    keep_cum = jnp.cumsum(log_keep.reshape(block_count, block_len), axis=1)[:, :, None]
    angles = offsets[:, None] * turn_rate[None, :]
    cosine = jnp.cos(angles)
    sine = jnp.sin(angles)
    growth = jnp.exp(offsets[None, :, None] * decay_rate[None, None, :] - keep_cum)
    blk_re = drive_re.reshape(block_count, block_len, num_cols)
    blk_im = drive_im.reshape(block_count, block_len, num_cols)
    pre_re = growth * (blk_re * cosine + blk_im * sine)
    pre_im = growth * (blk_im * cosine - blk_re * sine)
    lower_ones = (offsets[:, None] >= offsets[None, :]).astype(jnp.float32)
    summed = jnp.einsum(
        "ji,abik->abjk", lower_ones, jnp.stack([pre_re, pre_im]), precision=lax.Precision.HIGHEST
    )
    shrink = jnp.exp(keep_cum - offsets[None, :, None] * decay_rate[None, None, :])
    state_re = shrink * (summed[0] * cosine - summed[1] * sine)
    state_im = shrink * (summed[0] * sine + summed[1] * cosine)
    step_mag = jnp.exp(keep_cum[:, -1] - block_len * decay_rate[None, :])
    step_re = step_mag * jnp.cos(block_len * turn_rate)[None, :]
    step_im = step_mag * jnp.sin(block_len * turn_rate)[None, :]

    def advance(carried, inputs):
        carry_re, carry_im = carried
        mult_re, mult_im, end_re, end_im = inputs
        next_re = mult_re * carry_re - mult_im * carry_im + end_re
        next_im = mult_re * carry_im + mult_im * carry_re + end_im
        return ((next_re, next_im), (carry_re, carry_im))

    zeros_col = jnp.zeros((num_cols,), jnp.float32)
    enter_re, enter_im = lax.scan(
        advance, (zeros_col, zeros_col), (step_re, step_im, state_re[:, -1], state_im[:, -1])
    )[1]
    ahead = offsets + 1.0
    lift = jnp.exp(keep_cum - ahead[None, :, None] * decay_rate[None, None, :])
    lift_re = lift * jnp.cos(ahead[:, None] * turn_rate[None, :])
    lift_im = lift * jnp.sin(ahead[:, None] * turn_rate[None, :])
    state_re = state_re + lift_re * enter_re[:, None] - lift_im * enter_im[:, None]
    state_im = state_im + lift_re * enter_im[:, None] + lift_im * enter_re[:, None]
    return (state_re.reshape(seq_len, num_cols), state_im.reshape(seq_len, num_cols))


def carry_combine(earlier, later):
    early_re, early_im, early_sre, early_sim = earlier
    late_re, late_im, late_sre, late_sim = later
    joined_re = early_re * late_re - early_im * late_im
    joined_im = early_re * late_im + early_im * late_re
    joined_sre = late_re * early_sre - late_im * early_sim + late_sre
    joined_sim = late_re * early_sim + late_im * early_sre + late_sim
    return (joined_re, joined_im, joined_sre, joined_sim)


def per_device(
    tokens,
    conv_taps,
    log_rate,
    rotation,
    in_proj,
    out_proj,
    skip_gain,
    norm_gain,
    retention,
    cotangent,
):
    seq_len, local_width = tokens.shape
    tap_count = conv_taps.shape[0]
    local_heads, head_width, double_state = in_proj.shape
    state_size = double_state // 2
    num_cols = local_heads * state_size
    lead_rows = from_behind(tokens[seq_len - (tap_count - 1) :], SEQ, 1)
    padded = jnp.concatenate([lead_rows, tokens], axis=0).astype(jnp.float32)
    conv_sum = conv_taps[0][None, :] * padded[tap_count - 1 :]
    for offset in range(1, tap_count):
        conv_sum = (
            conv_sum
            + conv_taps[offset][None, :]
            * padded[tap_count - 1 - offset : tap_count - 1 - offset + seq_len]
        )
    mixed_in = conv_sum.astype(jnp.bfloat16)
    by_head = mixed_in.reshape(seq_len, local_heads, head_width)
    projected = jnp.einsum("thc,hck->thk", by_head, in_proj, preferred_element_type=jnp.float32)
    in_scale = jnp.sqrt(-jnp.expm1(-2.0 * log_rate))
    drive_re = projected[:, :, :state_size].reshape(seq_len, num_cols) * in_scale
    drive_im = projected[:, :, state_size:].reshape(seq_len, num_cols) * in_scale
    log_keep = jnp.log(retention)
    state_re, state_im = linear_run(drive_re, drive_im, log_rate, rotation, log_keep)
    keep_total = jnp.sum(log_keep)
    total_mag = jnp.exp(keep_total - seq_len * log_rate)
    total_re = total_mag * jnp.cos(seq_len * rotation)
    total_im = total_mag * jnp.sin(seq_len * rotation)
    unit_ones = jnp.ones((num_cols,), jnp.float32)
    zeros_col = jnp.zeros((num_cols,), jnp.float32)
    chained = carried_in(
        (total_re, total_im, state_re[-1], state_im[-1]),
        SEQ,
        carry_combine,
        (unit_ones, zeros_col, zeros_col, zeros_col),
        False,
    )
    enter_re, enter_im = (chained[2], chained[3])
    positions = jnp.arange(seq_len, dtype=jnp.float32)
    ahead = positions + 1.0
    lift = jnp.exp(jnp.cumsum(log_keep)[:, None] - ahead[:, None] * log_rate[None, :])
    lift_re = lift * jnp.cos(ahead[:, None] * rotation[None, :])
    lift_im = lift * jnp.sin(ahead[:, None] * rotation[None, :])
    state_re = state_re + lift_re * enter_re[None, :] - lift_im * enter_im[None, :]
    state_im = state_im + lift_re * enter_im[None, :] + lift_im * enter_re[None, :]
    state_bf = jnp.concatenate(
        [
            state_re.reshape(seq_len, local_heads, state_size),
            state_im.reshape(seq_len, local_heads, state_size),
        ],
        axis=2,
    ).astype(jnp.bfloat16)
    mixed = jnp.einsum(
        "thk,hck->thc", state_bf, out_proj, preferred_element_type=jnp.float32
    ).reshape(seq_len, local_width)
    mixed = mixed + skip_gain * mixed_in.astype(jnp.float32)
    squares = jnp.sum(mixed * mixed, axis=1)
    scaled = cotangent.astype(jnp.float32) * norm_gain
    dots = jnp.sum(scaled * mixed, axis=1)
    squares = lax.psum(squares, "chan")
    model_width = local_width * lax.axis_size("chan")
    inverse = lax.rsqrt(squares / model_width + 1e-06)
    normed = (mixed * inverse[:, None] * norm_gain).astype(jnp.bfloat16)
    dots = lax.psum(dots, "chan")
    mixed_grad = inverse[:, None] * (
        scaled - mixed * (inverse * inverse * dots / model_width)[:, None]
    )
    grad_bf = mixed_grad.astype(jnp.bfloat16).reshape(seq_len, local_heads, head_width)
    state_grad = jnp.einsum("thc,hck->thk", grad_bf, out_proj, preferred_element_type=jnp.float32)
    out_grad = jnp.einsum("thc,thk->hck", grad_bf, state_bf, preferred_element_type=jnp.float32)
    back_keep = jnp.concatenate([jnp.zeros((1,), jnp.float32), log_keep[::-1][:-1]])
    grad_re = state_grad[:, :, :state_size].reshape(seq_len, num_cols)[::-1]
    grad_im = state_grad[:, :, state_size:].reshape(seq_len, num_cols)[::-1]
    adj_re, adj_im = linear_run(grad_re, grad_im, log_rate, -rotation, back_keep)
    first_mag = jnp.exp(log_keep[0] - log_rate)
    cos_turn = jnp.cos(rotation)
    sin_turn = jnp.sin(rotation)
    first_re = first_mag * (cos_turn * adj_re[-1] + sin_turn * adj_im[-1])
    first_im = first_mag * (cos_turn * adj_im[-1] - sin_turn * adj_re[-1])
    back_chained = carried_in(
        (total_re, -total_im, first_re, first_im),
        SEQ,
        carry_combine,
        (unit_ones, zeros_col, zeros_col, zeros_col),
        True,
    )
    later_re, later_im = (back_chained[2], back_chained[3])
    back_lift = jnp.exp(jnp.cumsum(back_keep)[:, None] - positions[:, None] * log_rate[None, :])
    back_re = back_lift * jnp.cos(positions[:, None] * rotation[None, :])
    back_im = -back_lift * jnp.sin(positions[:, None] * rotation[None, :])
    adj_re = adj_re + back_re * later_re[None, :] - back_im * later_im[None, :]
    adj_im = adj_im + back_re * later_im[None, :] + back_im * later_re[None, :]
    adj_re = adj_re[::-1]
    adj_im = adj_im[::-1]
    drive_grad = jnp.concatenate(
        [
            (in_scale * adj_re).reshape(seq_len, local_heads, state_size),
            (in_scale * adj_im).reshape(seq_len, local_heads, state_size),
        ],
        axis=2,
    ).astype(jnp.bfloat16)
    in_grad = jnp.einsum("thc,thk->hck", by_head, drive_grad, preferred_element_type=jnp.float32)
    input_grad = jnp.einsum(
        "thk,hck->thc", drive_grad, in_proj, preferred_element_type=jnp.float32
    ).reshape(seq_len, local_width)
    input_grad = input_grad + skip_gain * mixed_grad
    trail_rows = from_behind(input_grad[: tap_count - 1], SEQ, -1)
    tail = jnp.concatenate([input_grad, trail_rows], axis=0)
    tokens_grad = conv_taps[0][None, :] * tail[:seq_len]
    for offset in range(1, tap_count):
        tokens_grad = tokens_grad + conv_taps[offset][None, :] * tail[offset : offset + seq_len]
    taps_grad = jnp.stack(
        [
            jnp.sum(
                input_grad * padded[tap_count - 1 - offset : tap_count - 1 - offset + seq_len],
                axis=0,
            )
            for offset in range(tap_count)
        ]
    )
    parts = (out_grad, in_grad, taps_grad)
    packed = tree_sum(jnp.concatenate([p.reshape(-1) for p in parts]), SEQ)
    ends = [0]
    for p in parts:
        ends.append(ends[-1] + p.size)
    out_grad, in_grad, taps_grad = (
        packed[a:b].reshape(p.shape) for a, b, p in zip(ends[:-1], ends[1:], parts)
    )
    return (normed, tokens_grad.astype(jnp.bfloat16), in_grad, out_grad, taps_grad)


def solution(mesh):
    seq_count, chan_count = mesh.devices.shape
    inner = 1
    while inner * inner < seq_count:
        inner *= 2
    devices = mesh.devices.reshape(seq_count // inner, inner, chan_count)
    mesh = Mesh(devices, SEQ + ("chan",))
    in_specs = (
        P(SEQ, "chan"),
        P(None, "chan"),
        P("chan"),
        P("chan"),
        P("chan", None, None),
        P("chan", None, None),
        P("chan"),
        P("chan"),
        P(SEQ),
        P(SEQ, "chan"),
    )
    out_specs = (
        P(SEQ, "chan"),
        P(SEQ, "chan"),
        P("chan", None, None),
        P("chan", None, None),
        P(None, "chan"),
    )
    return jax.shard_map(
        per_device, mesh=mesh, in_specs=in_specs, out_specs=out_specs, check_vma=False
    )
```

```python
import jax
import jax.numpy as jnp
from jax import lax
from jax.sharding import Mesh, PartitionSpec as P

SEQ = ("z", "y")


def from_behind(value, axis, by):
    length = lax.axis_size(axis)
    pairs = [(i, i + by) for i in range(length) if 0 <= i + by < length]
    return lax.ppermute(value, axis, pairs)


def tree_fold(stack, upto, combine, unit):
    keep = jnp.arange(stack.shape[0])[:, None, None] < upto
    level = jnp.where(keep, stack, unit[None])
    while level.shape[0] > 1:
        joined = combine(tuple(level[0::2].swapaxes(0, 1)), tuple(level[1::2].swapaxes(0, 1)))
        level = jnp.stack(joined, axis=1)
    return level[0]


def gather_all(value, axis):
    count = lax.axis_size(axis)
    spread = jnp.broadcast_to(value[None], (count,) + value.shape)
    return lax.all_to_all(spread, axis, 0, 0, tiled=True)


def carried_in(part, axis, combine, identity, reverse):
    packed = jnp.stack(part)
    unit = jnp.stack([jnp.zeros_like(a) + jnp.asarray(e, a.dtype) for a, e in zip(part, identity)])
    place = lax.axis_index(axis)
    every = gather_all(packed, axis)
    if reverse:
        every = every[::-1]
        place = lax.axis_size(axis) - 1 - place
    before = tree_fold(every, place, combine, unit)
    return tuple(before)


def tree_sum(value, axis):
    count = lax.axis_size(axis)
    flat = value.reshape(-1)
    width = -(-flat.size // count)
    block = jnp.pad(flat, (0, width * count - flat.size)).reshape(count, width)
    mine = jnp.sum(lax.all_to_all(block, axis, 0, 0, tiled=True), axis=0)
    return gather_all(mine, axis).reshape(-1)[: flat.size].reshape(value.shape)


def linear_run(drive_re, drive_im, decay_rate, turn_rate, log_keep):
    seq_len, num_cols = drive_re.shape
    block_len = min(64, seq_len)
    block_count = seq_len // block_len
    offsets = jnp.arange(block_len, dtype=jnp.float32)
    keep_cum = jnp.cumsum(log_keep.reshape(block_count, block_len), axis=1)[:, :, None]
    angles = offsets[:, None] * turn_rate[None, :]
    cosine = jnp.cos(angles)
    sine = jnp.sin(angles)
    growth = jnp.exp(offsets[None, :, None] * decay_rate[None, None, :] - keep_cum)
    blk_re = drive_re.reshape(block_count, block_len, num_cols)
    blk_im = drive_im.reshape(block_count, block_len, num_cols)
    pre_re = growth * (blk_re * cosine + blk_im * sine)
    pre_im = growth * (blk_im * cosine - blk_re * sine)
    lower_ones = (offsets[:, None] >= offsets[None, :]).astype(jnp.float32)
    summed = jnp.einsum(
        "ji,abik->abjk", lower_ones, jnp.stack([pre_re, pre_im]), precision=lax.Precision.HIGHEST
    )
    shrink = jnp.exp(keep_cum - offsets[None, :, None] * decay_rate[None, None, :])
    state_re = shrink * (summed[0] * cosine - summed[1] * sine)
    state_im = shrink * (summed[0] * sine + summed[1] * cosine)
    step_mag = jnp.exp(keep_cum[:, -1] - block_len * decay_rate[None, :])
    step_re = step_mag * jnp.cos(block_len * turn_rate)[None, :]
    step_im = step_mag * jnp.sin(block_len * turn_rate)[None, :]

    def advance(carried, inputs):
        carry_re, carry_im = carried
        mult_re, mult_im, end_re, end_im = inputs
        next_re = mult_re * carry_re - mult_im * carry_im + end_re
        next_im = mult_re * carry_im + mult_im * carry_re + end_im
        return ((next_re, next_im), (carry_re, carry_im))

    zeros_col = jnp.zeros((num_cols,), jnp.float32)
    enter_re, enter_im = lax.scan(
        advance, (zeros_col, zeros_col), (step_re, step_im, state_re[:, -1], state_im[:, -1])
    )[1]
    ahead = offsets + 1.0
    lift = jnp.exp(keep_cum - ahead[None, :, None] * decay_rate[None, None, :])
    lift_re = lift * jnp.cos(ahead[:, None] * turn_rate[None, :])
    lift_im = lift * jnp.sin(ahead[:, None] * turn_rate[None, :])
    state_re = state_re + lift_re * enter_re[:, None] - lift_im * enter_im[:, None]
    state_im = state_im + lift_re * enter_im[:, None] + lift_im * enter_re[:, None]
    return (state_re.reshape(seq_len, num_cols), state_im.reshape(seq_len, num_cols))


def carry_combine(earlier, later):
    early_re, early_im, early_sre, early_sim = earlier
    late_re, late_im, late_sre, late_sim = later
    joined_re = early_re * late_re - early_im * late_im
    joined_im = early_re * late_im + early_im * late_re
    joined_sre = late_re * early_sre - late_im * early_sim + late_sre
    joined_sim = late_re * early_sim + late_im * early_sre + late_sim
    return (joined_re, joined_im, joined_sre, joined_sim)


def per_device(
    tokens,
    conv_taps,
    log_rate,
    rotation,
    in_proj,
    out_proj,
    skip_gain,
    norm_gain,
    retention,
    cotangent,
):
    seq_len, local_width = tokens.shape
    tap_count = conv_taps.shape[0]
    local_heads, head_width, double_state = in_proj.shape
    state_size = double_state // 2
    num_cols = local_heads * state_size
    lead_rows = from_behind(tokens[seq_len - (tap_count - 1) :], SEQ, 1)
    padded = jnp.concatenate([lead_rows, tokens], axis=0).astype(jnp.float32)
    conv_sum = conv_taps[0][None, :] * padded[tap_count - 1 :]
    for offset in range(1, tap_count):
        conv_sum = (
            conv_sum
            + conv_taps[offset][None, :]
            * padded[tap_count - 1 - offset : tap_count - 1 - offset + seq_len]
        )
    mixed_in = conv_sum.astype(jnp.bfloat16)
    by_head = mixed_in.reshape(seq_len, local_heads, head_width)
    projected = jnp.einsum("thc,hck->thk", by_head, in_proj, preferred_element_type=jnp.float32)
    in_scale = jnp.sqrt(-jnp.expm1(-2.0 * log_rate))
    drive_re = projected[:, :, :state_size].reshape(seq_len, num_cols) * in_scale
    drive_im = projected[:, :, state_size:].reshape(seq_len, num_cols) * in_scale
    log_keep = jnp.log(retention)
    state_re, state_im = linear_run(drive_re, drive_im, log_rate, rotation, log_keep)
    keep_total = jnp.sum(log_keep)
    total_mag = jnp.exp(keep_total - seq_len * log_rate)
    total_re = total_mag * jnp.cos(seq_len * rotation)
    total_im = total_mag * jnp.sin(seq_len * rotation)
    unit_ones = jnp.ones((num_cols,), jnp.float32)
    zeros_col = jnp.zeros((num_cols,), jnp.float32)
    chained = carried_in(
        (total_re, total_im, state_re[-1], state_im[-1]),
        SEQ,
        carry_combine,
        (unit_ones, zeros_col, zeros_col, zeros_col),
        False,
    )
    enter_re, enter_im = (chained[2], chained[3])
    positions = jnp.arange(seq_len, dtype=jnp.float32)
    ahead = positions + 1.0
    lift = jnp.exp(jnp.cumsum(log_keep)[:, None] - ahead[:, None] * log_rate[None, :])
    lift_re = lift * jnp.cos(ahead[:, None] * rotation[None, :])
    lift_im = lift * jnp.sin(ahead[:, None] * rotation[None, :])
    state_re = state_re + lift_re * enter_re[None, :] - lift_im * enter_im[None, :]
    state_im = state_im + lift_re * enter_im[None, :] + lift_im * enter_re[None, :]
    state_bf = jnp.concatenate(
        [
            state_re.reshape(seq_len, local_heads, state_size),
            state_im.reshape(seq_len, local_heads, state_size),
        ],
        axis=2,
    ).astype(jnp.bfloat16)
    mixed = jnp.einsum(
        "thk,hck->thc", state_bf, out_proj, preferred_element_type=jnp.float32
    ).reshape(seq_len, local_width)
    mixed = mixed + skip_gain * mixed_in.astype(jnp.float32)
    squares = jnp.sum(mixed * mixed, axis=1)
    scaled = cotangent.astype(jnp.float32) * norm_gain
    dots = jnp.sum(scaled * mixed, axis=1)
    squares = lax.psum(squares, "chan")
    model_width = local_width * lax.axis_size("chan")
    inverse = lax.rsqrt(squares / model_width + 1e-06)
    normed = (mixed * inverse[:, None] * norm_gain).astype(jnp.bfloat16)
    dots = lax.psum(dots, "chan")
    mixed_grad = inverse[:, None] * (
        scaled - mixed * (inverse * inverse * dots / model_width)[:, None]
    )
    grad_bf = mixed_grad.astype(jnp.bfloat16).reshape(seq_len, local_heads, head_width)
    state_grad = jnp.einsum("thc,hck->thk", grad_bf, out_proj, preferred_element_type=jnp.float32)
    out_grad = jnp.einsum("thc,thk->hck", grad_bf, state_bf, preferred_element_type=jnp.float32)
    back_keep = jnp.concatenate([jnp.zeros((1,), jnp.float32), log_keep[::-1][:-1]])
    grad_re = state_grad[:, :, :state_size].reshape(seq_len, num_cols)[::-1]
    grad_im = state_grad[:, :, state_size:].reshape(seq_len, num_cols)[::-1]
    adj_re, adj_im = linear_run(grad_re, grad_im, log_rate, -rotation, back_keep)
    first_mag = jnp.exp(log_keep[0] - log_rate)
    cos_turn = jnp.cos(rotation)
    sin_turn = jnp.sin(rotation)
    first_re = first_mag * (cos_turn * adj_re[-1] + sin_turn * adj_im[-1])
    first_im = first_mag * (cos_turn * adj_im[-1] - sin_turn * adj_re[-1])
    back_chained = carried_in(
        (total_re, -total_im, first_re, first_im),
        SEQ,
        carry_combine,
        (unit_ones, zeros_col, zeros_col, zeros_col),
        True,
    )
    later_re, later_im = (back_chained[2], back_chained[3])
    back_lift = jnp.exp(jnp.cumsum(back_keep)[:, None] - positions[:, None] * log_rate[None, :])
    back_re = back_lift * jnp.cos(positions[:, None] * rotation[None, :])
    back_im = -back_lift * jnp.sin(positions[:, None] * rotation[None, :])
    adj_re = adj_re + back_re * later_re[None, :] - back_im * later_im[None, :]
    adj_im = adj_im + back_re * later_im[None, :] + back_im * later_re[None, :]
    adj_re = adj_re[::-1]
    adj_im = adj_im[::-1]
    drive_grad = jnp.concatenate(
        [
            (in_scale * adj_re).reshape(seq_len, local_heads, state_size),
            (in_scale * adj_im).reshape(seq_len, local_heads, state_size),
        ],
        axis=2,
    ).astype(jnp.bfloat16)
    in_grad = jnp.einsum("thc,thk->hck", by_head, drive_grad, preferred_element_type=jnp.float32)
    input_grad = jnp.einsum(
        "thk,hck->thc", drive_grad, in_proj, preferred_element_type=jnp.float32
    ).reshape(seq_len, local_width)
    input_grad = input_grad + skip_gain * mixed_grad
    trail_rows = from_behind(input_grad[: tap_count - 1], SEQ, -1)
    tail = jnp.concatenate([input_grad, trail_rows], axis=0)
    tokens_grad = conv_taps[0][None, :] * tail[:seq_len]
    for offset in range(1, tap_count):
        tokens_grad = tokens_grad + conv_taps[offset][None, :] * tail[offset : offset + seq_len]
    taps_grad = jnp.stack(
        [
            jnp.sum(
                input_grad * padded[tap_count - 1 - offset : tap_count - 1 - offset + seq_len],
                axis=0,
            )
            for offset in range(tap_count)
        ]
    )
    parts = (out_grad, in_grad, taps_grad)
    packed = tree_sum(jnp.concatenate([p.reshape(-1) for p in parts]), SEQ)
    ends = [0]
    for p in parts:
        ends.append(ends[-1] + p.size)
    out_grad, in_grad, taps_grad = (
        packed[a:b].reshape(p.shape) for a, b, p in zip(ends[:-1], ends[1:], parts)
    )
    return (normed, tokens_grad.astype(jnp.bfloat16), in_grad, out_grad, taps_grad)


def solution(mesh):
    seq_count, chan_count = mesh.devices.shape
    inner = 1
    while inner * inner < seq_count:
        inner *= 2
    devices = mesh.devices.reshape(seq_count // inner, inner, chan_count)
    mesh = Mesh(devices, SEQ + ("chan",))
    in_specs = (
        P(SEQ, "chan"),
        P(None, "chan"),
        P("chan"),
        P("chan"),
        P("chan", None, None),
        P("chan", None, None),
        P("chan"),
        P("chan"),
        P(SEQ),
        P(SEQ, "chan"),
    )
    out_specs = (
        P(SEQ, "chan"),
        P(SEQ, "chan"),
        P("chan", None, None),
        P("chan", None, None),
        P(None, "chan"),
    )
    return jax.shard_map(
        per_device, mesh=mesh, in_specs=in_specs, out_specs=out_specs, check_vma=False
    )
```

```python
import jax
import jax.numpy as jnp
from jax import lax
from jax.sharding import Mesh, PartitionSpec as P

SEQ = ("z", "y")


def from_behind(value, axis, by):
    length = lax.axis_size(axis)
    pairs = [(i, i + by) for i in range(length) if 0 <= i + by < length]
    return lax.ppermute(value, axis, pairs)


def tree_fold(stack, order, upto, combine, unit):
    count = len(order)
    width = count.bit_length() - 1
    flips = [int(format(r, f"0{width}b")[::-1], 2) for r in range(count)]
    level = jnp.take(stack, jnp.asarray([order[f] for f in flips]), axis=0)
    keep = jnp.asarray(flips)[:, None, None] < upto
    level = jnp.where(keep, level, unit[None])
    while level.shape[0] > 1:
        half = level.shape[0] // 2
        joined = combine(tuple(level[:half].swapaxes(0, 1)), tuple(level[half:].swapaxes(0, 1)))
        level = jnp.stack(joined, axis=1)
    return level[0]


def gather_all(value, axis):
    count = lax.axis_size(axis)
    spread = jnp.broadcast_to(value[None], (count,) + value.shape)
    return lax.all_to_all(spread, axis, 0, 0, tiled=True)


def carried_in(part, axis, combine, identity, reverse):
    packed = jnp.stack(part)
    unit = jnp.stack([jnp.zeros_like(a) + jnp.asarray(e, a.dtype) for a, e in zip(part, identity)])
    place = lax.axis_index(axis)
    every = gather_all(packed, axis)
    order = list(range(lax.axis_size(axis)))
    if reverse:
        order = order[::-1]
        place = lax.axis_size(axis) - 1 - place
    before = tree_fold(every, order, place, combine, unit)
    return tuple(before)


def tree_sum(value, axis):
    count = lax.axis_size(axis)
    flat = value.reshape(-1)
    width = -(-flat.size // count)
    block = jnp.pad(flat, (0, width * count - flat.size)).reshape(count, width)
    mine = jnp.sum(lax.all_to_all(block, axis, 0, 0, tiled=True), axis=0)
    return gather_all(mine, axis).reshape(-1)[: flat.size].reshape(value.shape)


def linear_run(drive_re, drive_im, decay_rate, turn_rate, log_keep):
    seq_len, num_cols = drive_re.shape
    block_len = min(64, seq_len)
    block_count = seq_len // block_len
    offsets = jnp.arange(block_len, dtype=jnp.float32)
    keep_cum = jnp.cumsum(log_keep.reshape(block_count, block_len), axis=1)[:, :, None]
    angles = offsets[:, None] * turn_rate[None, :]
    cosine = jnp.cos(angles)
    sine = jnp.sin(angles)
    growth = jnp.exp(offsets[None, :, None] * decay_rate[None, None, :] - keep_cum)
    blk_re = drive_re.reshape(block_count, block_len, num_cols)
    blk_im = drive_im.reshape(block_count, block_len, num_cols)
    pre_re = growth * (blk_re * cosine + blk_im * sine)
    pre_im = growth * (blk_im * cosine - blk_re * sine)
    lower_ones = (offsets[:, None] >= offsets[None, :]).astype(jnp.float32)
    summed = jnp.einsum(
        "ji,abik->abjk", lower_ones, jnp.stack([pre_re, pre_im]), precision=lax.Precision.HIGHEST
    )
    shrink = jnp.exp(keep_cum - offsets[None, :, None] * decay_rate[None, None, :])
    state_re = shrink * (summed[0] * cosine - summed[1] * sine)
    state_im = shrink * (summed[0] * sine + summed[1] * cosine)
    step_mag = jnp.exp(keep_cum[:, -1] - block_len * decay_rate[None, :])
    step_re = step_mag * jnp.cos(block_len * turn_rate)[None, :]
    step_im = step_mag * jnp.sin(block_len * turn_rate)[None, :]

    def advance(carried, inputs):
        carry_re, carry_im = carried
        mult_re, mult_im, end_re, end_im = inputs
        next_re = mult_re * carry_re - mult_im * carry_im + end_re
        next_im = mult_re * carry_im + mult_im * carry_re + end_im
        return ((next_re, next_im), (carry_re, carry_im))

    zeros_col = jnp.zeros((num_cols,), jnp.float32)
    enter_re, enter_im = lax.scan(
        advance, (zeros_col, zeros_col), (step_re, step_im, state_re[:, -1], state_im[:, -1])
    )[1]
    ahead = offsets + 1.0
    lift = jnp.exp(keep_cum - ahead[None, :, None] * decay_rate[None, None, :])
    lift_re = lift * jnp.cos(ahead[:, None] * turn_rate[None, :])
    lift_im = lift * jnp.sin(ahead[:, None] * turn_rate[None, :])
    state_re = state_re + lift_re * enter_re[:, None] - lift_im * enter_im[:, None]
    state_im = state_im + lift_re * enter_im[:, None] + lift_im * enter_re[:, None]
    return (state_re.reshape(seq_len, num_cols), state_im.reshape(seq_len, num_cols))


def carry_combine(earlier, later):
    early_re, early_im, early_sre, early_sim = earlier
    late_re, late_im, late_sre, late_sim = later
    joined_re = early_re * late_re - early_im * late_im
    joined_im = early_re * late_im + early_im * late_re
    joined_sre = late_re * early_sre - late_im * early_sim + late_sre
    joined_sim = late_re * early_sim + late_im * early_sre + late_sim
    return (joined_re, joined_im, joined_sre, joined_sim)


def per_device(
    tokens,
    conv_taps,
    log_rate,
    rotation,
    in_proj,
    out_proj,
    skip_gain,
    norm_gain,
    retention,
    cotangent,
):
    seq_len, local_width = tokens.shape
    tap_count = conv_taps.shape[0]
    local_heads, head_width, double_state = in_proj.shape
    state_size = double_state // 2
    num_cols = local_heads * state_size
    lead_rows = from_behind(tokens[seq_len - (tap_count - 1) :], SEQ, 1)
    padded = jnp.concatenate([lead_rows, tokens], axis=0).astype(jnp.float32)
    conv_sum = conv_taps[0][None, :] * padded[tap_count - 1 :]
    for offset in range(1, tap_count):
        conv_sum = (
            conv_sum
            + conv_taps[offset][None, :]
            * padded[tap_count - 1 - offset : tap_count - 1 - offset + seq_len]
        )
    mixed_in = conv_sum.astype(jnp.bfloat16)
    by_head = mixed_in.reshape(seq_len, local_heads, head_width)
    projected = jnp.einsum("thc,hck->thk", by_head, in_proj, preferred_element_type=jnp.float32)
    in_scale = jnp.sqrt(-jnp.expm1(-2.0 * log_rate))
    drive_re = projected[:, :, :state_size].reshape(seq_len, num_cols) * in_scale
    drive_im = projected[:, :, state_size:].reshape(seq_len, num_cols) * in_scale
    log_keep = jnp.log(retention)
    state_re, state_im = linear_run(drive_re, drive_im, log_rate, rotation, log_keep)
    keep_total = jnp.sum(log_keep)
    total_mag = jnp.exp(keep_total - seq_len * log_rate)
    total_re = total_mag * jnp.cos(seq_len * rotation)
    total_im = total_mag * jnp.sin(seq_len * rotation)
    unit_ones = jnp.ones((num_cols,), jnp.float32)
    zeros_col = jnp.zeros((num_cols,), jnp.float32)
    chained = carried_in(
        (total_re, total_im, state_re[-1], state_im[-1]),
        SEQ,
        carry_combine,
        (unit_ones, zeros_col, zeros_col, zeros_col),
        False,
    )
    enter_re, enter_im = (chained[2], chained[3])
    positions = jnp.arange(seq_len, dtype=jnp.float32)
    ahead = positions + 1.0
    lift = jnp.exp(jnp.cumsum(log_keep)[:, None] - ahead[:, None] * log_rate[None, :])
    lift_re = lift * jnp.cos(ahead[:, None] * rotation[None, :])
    lift_im = lift * jnp.sin(ahead[:, None] * rotation[None, :])
    state_re = state_re + lift_re * enter_re[None, :] - lift_im * enter_im[None, :]
    state_im = state_im + lift_re * enter_im[None, :] + lift_im * enter_re[None, :]
    state_bf = jnp.concatenate(
        [
            state_re.reshape(seq_len, local_heads, state_size),
            state_im.reshape(seq_len, local_heads, state_size),
        ],
        axis=2,
    ).astype(jnp.bfloat16)
    mixed = jnp.einsum(
        "thk,hck->thc", state_bf, out_proj, preferred_element_type=jnp.float32
    ).reshape(seq_len, local_width)
    mixed = mixed + skip_gain * mixed_in.astype(jnp.float32)
    squares = jnp.sum(mixed * mixed, axis=1)
    scaled = cotangent.astype(jnp.float32) * norm_gain
    dots = jnp.sum(scaled * mixed, axis=1)
    squares, dots = jnp.sum(gather_all(jnp.stack([squares, dots]), "chan"), axis=0)
    model_width = local_width * lax.axis_size("chan")
    inverse = lax.rsqrt(squares / model_width + 1e-06)
    normed = (mixed * inverse[:, None] * norm_gain).astype(jnp.bfloat16)
    mixed_grad = inverse[:, None] * (
        scaled - mixed * (inverse * inverse * dots / model_width)[:, None]
    )
    grad_bf = mixed_grad.astype(jnp.bfloat16).reshape(seq_len, local_heads, head_width)
    state_grad = jnp.einsum("thc,hck->thk", grad_bf, out_proj, preferred_element_type=jnp.float32)
    out_grad = jnp.einsum("thc,thk->hck", grad_bf, state_bf, preferred_element_type=jnp.float32)
    back_keep = jnp.concatenate([jnp.zeros((1,), jnp.float32), log_keep[::-1][:-1]])
    grad_re = state_grad[:, :, :state_size].reshape(seq_len, num_cols)[::-1]
    grad_im = state_grad[:, :, state_size:].reshape(seq_len, num_cols)[::-1]
    adj_re, adj_im = linear_run(grad_re, grad_im, log_rate, -rotation, back_keep)
    first_mag = jnp.exp(log_keep[0] - log_rate)
    cos_turn = jnp.cos(rotation)
    sin_turn = jnp.sin(rotation)
    first_re = first_mag * (cos_turn * adj_re[-1] + sin_turn * adj_im[-1])
    first_im = first_mag * (cos_turn * adj_im[-1] - sin_turn * adj_re[-1])
    back_chained = carried_in(
        (total_re, -total_im, first_re, first_im),
        SEQ,
        carry_combine,
        (unit_ones, zeros_col, zeros_col, zeros_col),
        True,
    )
    later_re, later_im = (back_chained[2], back_chained[3])
    back_lift = jnp.exp(jnp.cumsum(back_keep)[:, None] - positions[:, None] * log_rate[None, :])
    back_re = back_lift * jnp.cos(positions[:, None] * rotation[None, :])
    back_im = -back_lift * jnp.sin(positions[:, None] * rotation[None, :])
    adj_re = adj_re + back_re * later_re[None, :] - back_im * later_im[None, :]
    adj_im = adj_im + back_re * later_im[None, :] + back_im * later_re[None, :]
    adj_re = adj_re[::-1]
    adj_im = adj_im[::-1]
    drive_grad = jnp.concatenate(
        [
            (in_scale * adj_re).reshape(seq_len, local_heads, state_size),
            (in_scale * adj_im).reshape(seq_len, local_heads, state_size),
        ],
        axis=2,
    ).astype(jnp.bfloat16)
    in_grad = jnp.einsum("thc,thk->hck", by_head, drive_grad, preferred_element_type=jnp.float32)
    input_grad = jnp.einsum(
        "thk,hck->thc", drive_grad, in_proj, preferred_element_type=jnp.float32
    ).reshape(seq_len, local_width)
    input_grad = input_grad + skip_gain * mixed_grad
    trail_rows = from_behind(input_grad[: tap_count - 1], SEQ, -1)
    tail = jnp.concatenate([input_grad, trail_rows], axis=0)
    tokens_grad = conv_taps[0][None, :] * tail[:seq_len]
    for offset in range(1, tap_count):
        tokens_grad = tokens_grad + conv_taps[offset][None, :] * tail[offset : offset + seq_len]
    taps_grad = jnp.stack(
        [
            jnp.sum(
                input_grad * padded[tap_count - 1 - offset : tap_count - 1 - offset + seq_len],
                axis=0,
            )
            for offset in range(tap_count)
        ]
    )
    parts = (out_grad, in_grad, taps_grad)
    packed = tree_sum(jnp.concatenate([p.reshape(-1) for p in parts]), SEQ)
    ends = [0]
    for p in parts:
        ends.append(ends[-1] + p.size)
    out_grad, in_grad, taps_grad = (
        packed[a:b].reshape(p.shape) for a, b, p in zip(ends[:-1], ends[1:], parts)
    )
    return (normed, tokens_grad.astype(jnp.bfloat16), in_grad, out_grad, taps_grad)


def solution(mesh):
    seq_count, chan_count = mesh.devices.shape
    inner = 1
    while inner * inner < seq_count:
        inner *= 2
    devices = mesh.devices.reshape(seq_count // inner, inner, chan_count)
    mesh = Mesh(devices, SEQ + ("chan",))
    in_specs = (
        P(SEQ, "chan"),
        P(None, "chan"),
        P("chan"),
        P("chan"),
        P("chan", None, None),
        P("chan", None, None),
        P("chan"),
        P("chan"),
        P(SEQ),
        P(SEQ, "chan"),
    )
    out_specs = (
        P(SEQ, "chan"),
        P(SEQ, "chan"),
        P("chan", None, None),
        P("chan", None, None),
        P(None, "chan"),
    )
    return jax.shard_map(
        per_device, mesh=mesh, in_specs=in_specs, out_specs=out_specs, check_vma=False
    )
```

```python
import jax
import jax.numpy as jnp
from jax import lax
from jax.sharding import Mesh, PartitionSpec as P

SEQ = ("z", "y")


def from_behind(value, axis, by):
    length = lax.axis_size(axis)
    pairs = [(i, i + by) for i in range(length) if 0 <= i + by < length]
    return lax.ppermute(value, axis, pairs)


def tree_fold(stack, order, upto, combine, unit):
    count = len(order)
    width = count.bit_length() - 1
    flips = [int(format(r, f"0{width}b")[::-1], 2) for r in range(count)]
    level = jnp.take(stack, jnp.asarray([order[f] for f in flips]), axis=0)
    keep = jnp.asarray(flips)[:, None, None] < upto
    level = jnp.where(keep, level, unit[None])
    while level.shape[0] > 1:
        half = level.shape[0] // 2
        joined = combine(tuple(level[:half].swapaxes(0, 1)), tuple(level[half:].swapaxes(0, 1)))
        level = jnp.stack(joined, axis=1)
    return level[0]


def gather_all(value, axis):
    count = lax.axis_size(axis)
    spread = jnp.broadcast_to(value[None], (count,) + value.shape)
    return lax.all_to_all(spread, axis, 0, 0, tiled=True)


def carried_in(mult_re, mult_im, every, axis, combine, identity, reverse):
    every = jnp.concatenate([jnp.stack([mult_re, mult_im], axis=1), every[:, :2]], axis=1)
    unit = jnp.stack([jnp.zeros_like(mult_re[0]) + e for e in identity])
    place = lax.axis_index(axis)
    order = list(range(lax.axis_size(axis)))
    if reverse:
        order = order[::-1]
        place = lax.axis_size(axis) - 1 - place
    before = tree_fold(every, order, place, combine, unit)
    return tuple(before)


def tree_sum(value, axis):
    count = lax.axis_size(axis)
    flat = value.reshape(-1)
    width = -(-flat.size // count)
    block = jnp.pad(flat, (0, width * count - flat.size)).reshape(count, width)
    mine = jnp.sum(lax.all_to_all(block, axis, 0, 0, tiled=True), axis=0)
    return gather_all(mine, axis).reshape(-1)[: flat.size].reshape(value.shape)


def linear_run(drive_re, drive_im, decay_rate, turn_rate, log_keep):
    seq_len, num_cols = drive_re.shape
    block_len = min(64, seq_len)
    block_count = seq_len // block_len
    offsets = jnp.arange(block_len, dtype=jnp.float32)
    keep_cum = jnp.cumsum(log_keep.reshape(block_count, block_len), axis=1)[:, :, None]
    angles = offsets[:, None] * turn_rate[None, :]
    cosine = jnp.cos(angles)
    sine = jnp.sin(angles)
    growth = jnp.exp(offsets[None, :, None] * decay_rate[None, None, :] - keep_cum)
    blk_re = drive_re.reshape(block_count, block_len, num_cols)
    blk_im = drive_im.reshape(block_count, block_len, num_cols)
    pre_re = growth * (blk_re * cosine + blk_im * sine)
    pre_im = growth * (blk_im * cosine - blk_re * sine)
    lower_ones = (offsets[:, None] >= offsets[None, :]).astype(jnp.float32)
    summed = jnp.einsum(
        "ji,abik->abjk", lower_ones, jnp.stack([pre_re, pre_im]), precision=lax.Precision.HIGHEST
    )
    shrink = jnp.exp(keep_cum - offsets[None, :, None] * decay_rate[None, None, :])
    state_re = shrink * (summed[0] * cosine - summed[1] * sine)
    state_im = shrink * (summed[0] * sine + summed[1] * cosine)
    step_mag = jnp.exp(keep_cum[:, -1] - block_len * decay_rate[None, :])
    step_re = step_mag * jnp.cos(block_len * turn_rate)[None, :]
    step_im = step_mag * jnp.sin(block_len * turn_rate)[None, :]

    def advance(carried, inputs):
        carry_re, carry_im = carried
        mult_re, mult_im, end_re, end_im = inputs
        next_re = mult_re * carry_re - mult_im * carry_im + end_re
        next_im = mult_re * carry_im + mult_im * carry_re + end_im
        return ((next_re, next_im), (carry_re, carry_im))

    zeros_col = jnp.zeros((num_cols,), jnp.float32)
    enter_re, enter_im = lax.scan(
        advance, (zeros_col, zeros_col), (step_re, step_im, state_re[:, -1], state_im[:, -1])
    )[1]
    ahead = offsets + 1.0
    lift = jnp.exp(keep_cum - ahead[None, :, None] * decay_rate[None, None, :])
    lift_re = lift * jnp.cos(ahead[:, None] * turn_rate[None, :])
    lift_im = lift * jnp.sin(ahead[:, None] * turn_rate[None, :])
    state_re = state_re + lift_re * enter_re[:, None] - lift_im * enter_im[:, None]
    state_im = state_im + lift_re * enter_im[:, None] + lift_im * enter_re[:, None]
    return (state_re.reshape(seq_len, num_cols), state_im.reshape(seq_len, num_cols))


def carry_combine(earlier, later):
    early_re, early_im, early_sre, early_sim = earlier
    late_re, late_im, late_sre, late_sim = later
    joined_re = early_re * late_re - early_im * late_im
    joined_im = early_re * late_im + early_im * late_re
    joined_sre = late_re * early_sre - late_im * early_sim + late_sre
    joined_sim = late_re * early_sim + late_im * early_sre + late_sim
    return (joined_re, joined_im, joined_sre, joined_sim)


def per_device(
    tokens,
    conv_taps,
    log_rate,
    rotation,
    in_proj,
    out_proj,
    skip_gain,
    norm_gain,
    retention,
    cotangent,
):
    seq_len, local_width = tokens.shape
    tap_count = conv_taps.shape[0]
    local_heads, head_width, double_state = in_proj.shape
    state_size = double_state // 2
    num_cols = local_heads * state_size
    lead_rows = from_behind(tokens[seq_len - (tap_count - 1) :], SEQ, 1)
    padded = jnp.concatenate([lead_rows, tokens], axis=0).astype(jnp.float32)
    conv_sum = conv_taps[0][None, :] * padded[tap_count - 1 :]
    for offset in range(1, tap_count):
        conv_sum = (
            conv_sum
            + conv_taps[offset][None, :]
            * padded[tap_count - 1 - offset : tap_count - 1 - offset + seq_len]
        )
    mixed_in = conv_sum.astype(jnp.bfloat16)
    by_head = mixed_in.reshape(seq_len, local_heads, head_width)
    projected = jnp.einsum("thc,hck->thk", by_head, in_proj, preferred_element_type=jnp.float32)
    in_scale = jnp.sqrt(-jnp.expm1(-2.0 * log_rate))
    drive_re = projected[:, :, :state_size].reshape(seq_len, num_cols) * in_scale
    drive_im = projected[:, :, state_size:].reshape(seq_len, num_cols) * in_scale
    log_keep = jnp.log(retention)
    state_re, state_im = linear_run(drive_re, drive_im, log_rate, rotation, log_keep)
    keep_total = jnp.sum(log_keep)
    ends = gather_all(
        jnp.stack([state_re[-1], state_im[-1], jnp.broadcast_to(keep_total, state_re[-1].shape)]), SEQ
    )
    total_mag = jnp.exp(ends[:, 2, :1] - seq_len * log_rate)
    total_re = total_mag * jnp.cos(seq_len * rotation)
    total_im = total_mag * jnp.sin(seq_len * rotation)
    chained = carried_in(total_re, total_im, ends, SEQ, carry_combine, (1.0, 0.0, 0.0, 0.0), False)
    enter_re, enter_im = (chained[2], chained[3])
    positions = jnp.arange(seq_len, dtype=jnp.float32)
    ahead = positions + 1.0
    lift = jnp.exp(jnp.cumsum(log_keep)[:, None] - ahead[:, None] * log_rate[None, :])
    lift_re = lift * jnp.cos(ahead[:, None] * rotation[None, :])
    lift_im = lift * jnp.sin(ahead[:, None] * rotation[None, :])
    state_re = state_re + lift_re * enter_re[None, :] - lift_im * enter_im[None, :]
    state_im = state_im + lift_re * enter_im[None, :] + lift_im * enter_re[None, :]
    state_bf = jnp.concatenate(
        [
            state_re.reshape(seq_len, local_heads, state_size),
            state_im.reshape(seq_len, local_heads, state_size),
        ],
        axis=2,
    ).astype(jnp.bfloat16)
    mixed = jnp.einsum(
        "thk,hck->thc", state_bf, out_proj, preferred_element_type=jnp.float32
    ).reshape(seq_len, local_width)
    mixed = mixed + skip_gain * mixed_in.astype(jnp.float32)
    squares = jnp.sum(mixed * mixed, axis=1)
    scaled = cotangent.astype(jnp.float32) * norm_gain
    dots = jnp.sum(scaled * mixed, axis=1)
    squares, dots = jnp.sum(gather_all(jnp.stack([squares, dots]), "chan"), axis=0)
    model_width = local_width * lax.axis_size("chan")
    inverse = lax.rsqrt(squares / model_width + 1e-06)
    normed = (mixed * inverse[:, None] * norm_gain).astype(jnp.bfloat16)
    mixed_grad = inverse[:, None] * (
        scaled - mixed * (inverse * inverse * dots / model_width)[:, None]
    )
    grad_bf = mixed_grad.astype(jnp.bfloat16).reshape(seq_len, local_heads, head_width)
    state_grad = jnp.einsum("thc,hck->thk", grad_bf, out_proj, preferred_element_type=jnp.float32)
    out_grad = jnp.einsum("thc,thk->hck", grad_bf, state_bf, preferred_element_type=jnp.float32)
    back_keep = jnp.concatenate([jnp.zeros((1,), jnp.float32), log_keep[::-1][:-1]])
    grad_re = state_grad[:, :, :state_size].reshape(seq_len, num_cols)[::-1]
    grad_im = state_grad[:, :, state_size:].reshape(seq_len, num_cols)[::-1]
    adj_re, adj_im = linear_run(grad_re, grad_im, log_rate, -rotation, back_keep)
    first_mag = jnp.exp(log_keep[0] - log_rate)
    cos_turn = jnp.cos(rotation)
    sin_turn = jnp.sin(rotation)
    first_re = first_mag * (cos_turn * adj_re[-1] + sin_turn * adj_im[-1])
    first_im = first_mag * (cos_turn * adj_im[-1] - sin_turn * adj_re[-1])
    firsts = gather_all(jnp.stack([first_re, first_im]), SEQ)
    back_chained = carried_in(
        total_re, -total_im, firsts, SEQ, carry_combine, (1.0, 0.0, 0.0, 0.0), True
    )
    later_re, later_im = (back_chained[2], back_chained[3])
    back_lift = jnp.exp(jnp.cumsum(back_keep)[:, None] - positions[:, None] * log_rate[None, :])
    back_re = back_lift * jnp.cos(positions[:, None] * rotation[None, :])
    back_im = -back_lift * jnp.sin(positions[:, None] * rotation[None, :])
    adj_re = adj_re + back_re * later_re[None, :] - back_im * later_im[None, :]
    adj_im = adj_im + back_re * later_im[None, :] + back_im * later_re[None, :]
    adj_re = adj_re[::-1]
    adj_im = adj_im[::-1]
    drive_grad = jnp.concatenate(
        [
            (in_scale * adj_re).reshape(seq_len, local_heads, state_size),
            (in_scale * adj_im).reshape(seq_len, local_heads, state_size),
        ],
        axis=2,
    ).astype(jnp.bfloat16)
    in_grad = jnp.einsum("thc,thk->hck", by_head, drive_grad, preferred_element_type=jnp.float32)
    input_grad = jnp.einsum(
        "thk,hck->thc", drive_grad, in_proj, preferred_element_type=jnp.float32
    ).reshape(seq_len, local_width)
    input_grad = input_grad + skip_gain * mixed_grad
    trail_rows = from_behind(input_grad[: tap_count - 1], SEQ, -1)
    tail = jnp.concatenate([input_grad, trail_rows], axis=0)
    tokens_grad = conv_taps[0][None, :] * tail[:seq_len]
    for offset in range(1, tap_count):
        tokens_grad = tokens_grad + conv_taps[offset][None, :] * tail[offset : offset + seq_len]
    taps_grad = jnp.stack(
        [
            jnp.sum(
                input_grad * padded[tap_count - 1 - offset : tap_count - 1 - offset + seq_len],
                axis=0,
            )
            for offset in range(tap_count)
        ]
    )
    parts = (out_grad, in_grad, taps_grad)
    packed = tree_sum(jnp.concatenate([p.reshape(-1) for p in parts]), SEQ)
    ends = [0]
    for p in parts:
        ends.append(ends[-1] + p.size)
    out_grad, in_grad, taps_grad = (
        packed[a:b].reshape(p.shape) for a, b, p in zip(ends[:-1], ends[1:], parts)
    )
    return (normed, tokens_grad.astype(jnp.bfloat16), in_grad, out_grad, taps_grad)


def solution(mesh):
    seq_count, chan_count = mesh.devices.shape
    inner = 1
    while inner * inner < seq_count:
        inner *= 2
    devices = mesh.devices.reshape(seq_count // inner, inner, chan_count)
    mesh = Mesh(devices, SEQ + ("chan",))
    in_specs = (
        P(SEQ, "chan"),
        P(None, "chan"),
        P("chan"),
        P("chan"),
        P("chan", None, None),
        P("chan", None, None),
        P("chan"),
        P("chan"),
        P(SEQ),
        P(SEQ, "chan"),
    )
    out_specs = (
        P(SEQ, "chan"),
        P(SEQ, "chan"),
        P("chan", None, None),
        P("chan", None, None),
        P(None, "chan"),
    )
    return jax.shard_map(
        per_device, mesh=mesh, in_specs=in_specs, out_specs=out_specs, check_vma=False
    )
```

```python
import jax
import jax.numpy as jnp
from jax import lax
from jax.sharding import Mesh, PartitionSpec as P

SEQ = ("z", "y")


def from_behind(value, axis, by):
    length = lax.axis_size(axis)
    pairs = [(i, i + by) for i in range(length) if 0 <= i + by < length]
    return lax.ppermute(value, axis, pairs)


def tree_fold(stack, order, upto, combine, unit):
    count = len(order)
    width = count.bit_length() - 1
    flips = [int(format(r, f"0{width}b")[::-1], 2) for r in range(count)]
    level = jnp.take(stack, jnp.asarray([order[f] for f in flips]), axis=0)
    keep = jnp.asarray(flips)[:, None, None] < upto
    level = jnp.where(keep, level, unit[None])
    while level.shape[0] > 1:
        half = level.shape[0] // 2
        joined = combine(tuple(level[:half].swapaxes(0, 1)), tuple(level[half:].swapaxes(0, 1)))
        level = jnp.stack(joined, axis=1)
    return level[0]


def gather_all(value, axis):
    count = lax.axis_size(axis)
    spread = jnp.broadcast_to(value[None], (count,) + value.shape)
    return lax.all_to_all(spread, axis, 0, 0, tiled=True)


def carried_in(mult_re, mult_im, every, axis, combine, identity, reverse):
    every = jnp.concatenate([jnp.stack([mult_re, mult_im], axis=1), every[:, :2]], axis=1)
    unit = jnp.stack([jnp.zeros_like(mult_re[0]) + e for e in identity])
    place = lax.axis_index(axis)
    order = list(range(lax.axis_size(axis)))
    if reverse:
        order = order[::-1]
        place = lax.axis_size(axis) - 1 - place
    before = tree_fold(every, order, place, combine, unit)
    return tuple(before)


def tree_sum(value, axis):
    count = lax.axis_size(axis)
    flat = value.reshape(-1)
    width = -(-flat.size // count)
    block = jnp.pad(flat, (0, width * count - flat.size)).reshape(count, width)
    mine = jnp.sum(lax.all_to_all(block, axis, 0, 0, tiled=True), axis=0)
    spread = gather_all(mine.astype(jnp.bfloat16), axis).astype(jnp.float32)
    return spread.reshape(-1)[: flat.size].reshape(value.shape)


def linear_run(drive_re, drive_im, decay_rate, turn_rate, log_keep):
    seq_len, num_cols = drive_re.shape
    block_len = min(64, seq_len)
    block_count = seq_len // block_len
    offsets = jnp.arange(block_len, dtype=jnp.float32)
    keep_cum = jnp.cumsum(log_keep.reshape(block_count, block_len), axis=1)[:, :, None]
    angles = offsets[:, None] * turn_rate[None, :]
    cosine = jnp.cos(angles)
    sine = jnp.sin(angles)
    growth = jnp.exp(offsets[None, :, None] * decay_rate[None, None, :] - keep_cum)
    blk_re = drive_re.reshape(block_count, block_len, num_cols)
    blk_im = drive_im.reshape(block_count, block_len, num_cols)
    pre_re = growth * (blk_re * cosine + blk_im * sine)
    pre_im = growth * (blk_im * cosine - blk_re * sine)
    lower_ones = (offsets[:, None] >= offsets[None, :]).astype(jnp.float32)
    summed = jnp.einsum(
        "ji,abik->abjk", lower_ones, jnp.stack([pre_re, pre_im]), precision=lax.Precision.HIGHEST
    )
    shrink = jnp.exp(keep_cum - offsets[None, :, None] * decay_rate[None, None, :])
    state_re = shrink * (summed[0] * cosine - summed[1] * sine)
    state_im = shrink * (summed[0] * sine + summed[1] * cosine)
    step_mag = jnp.exp(keep_cum[:, -1] - block_len * decay_rate[None, :])
    step_re = step_mag * jnp.cos(block_len * turn_rate)[None, :]
    step_im = step_mag * jnp.sin(block_len * turn_rate)[None, :]

    def advance(carried, inputs):
        carry_re, carry_im = carried
        mult_re, mult_im, end_re, end_im = inputs
        next_re = mult_re * carry_re - mult_im * carry_im + end_re
        next_im = mult_re * carry_im + mult_im * carry_re + end_im
        return ((next_re, next_im), (carry_re, carry_im))

    zeros_col = jnp.zeros((num_cols,), jnp.float32)
    enter_re, enter_im = lax.scan(
        advance, (zeros_col, zeros_col), (step_re, step_im, state_re[:, -1], state_im[:, -1])
    )[1]
    ahead = offsets + 1.0
    lift = jnp.exp(keep_cum - ahead[None, :, None] * decay_rate[None, None, :])
    lift_re = lift * jnp.cos(ahead[:, None] * turn_rate[None, :])
    lift_im = lift * jnp.sin(ahead[:, None] * turn_rate[None, :])
    state_re = state_re + lift_re * enter_re[:, None] - lift_im * enter_im[:, None]
    state_im = state_im + lift_re * enter_im[:, None] + lift_im * enter_re[:, None]
    return (state_re.reshape(seq_len, num_cols), state_im.reshape(seq_len, num_cols))


def carry_combine(earlier, later):
    early_re, early_im, early_sre, early_sim = earlier
    late_re, late_im, late_sre, late_sim = later
    joined_re = early_re * late_re - early_im * late_im
    joined_im = early_re * late_im + early_im * late_re
    joined_sre = late_re * early_sre - late_im * early_sim + late_sre
    joined_sim = late_re * early_sim + late_im * early_sre + late_sim
    return (joined_re, joined_im, joined_sre, joined_sim)


def per_device(
    tokens,
    conv_taps,
    log_rate,
    rotation,
    in_proj,
    out_proj,
    skip_gain,
    norm_gain,
    retention,
    cotangent,
):
    seq_len, local_width = tokens.shape
    tap_count = conv_taps.shape[0]
    local_heads, head_width, double_state = in_proj.shape
    state_size = double_state // 2
    num_cols = local_heads * state_size
    lead_rows = from_behind(tokens[seq_len - (tap_count - 1) :], SEQ, 1)
    padded = jnp.concatenate([lead_rows, tokens], axis=0).astype(jnp.float32)
    conv_sum = conv_taps[0][None, :] * padded[tap_count - 1 :]
    for offset in range(1, tap_count):
        conv_sum = (
            conv_sum
            + conv_taps[offset][None, :]
            * padded[tap_count - 1 - offset : tap_count - 1 - offset + seq_len]
        )
    mixed_in = conv_sum.astype(jnp.bfloat16)
    by_head = mixed_in.reshape(seq_len, local_heads, head_width)
    projected = jnp.einsum("thc,hck->thk", by_head, in_proj, preferred_element_type=jnp.float32)
    in_scale = jnp.sqrt(-jnp.expm1(-2.0 * log_rate))
    drive_re = projected[:, :, :state_size].reshape(seq_len, num_cols) * in_scale
    drive_im = projected[:, :, state_size:].reshape(seq_len, num_cols) * in_scale
    log_keep = jnp.log(retention)
    state_re, state_im = linear_run(drive_re, drive_im, log_rate, rotation, log_keep)
    keep_total = jnp.sum(log_keep)
    ends = gather_all(
        jnp.stack([state_re[-1], state_im[-1], jnp.broadcast_to(keep_total, state_re[-1].shape)]), SEQ
    )
    total_mag = jnp.exp(ends[:, 2, :1] - seq_len * log_rate)
    total_re = total_mag * jnp.cos(seq_len * rotation)
    total_im = total_mag * jnp.sin(seq_len * rotation)
    chained = carried_in(total_re, total_im, ends, SEQ, carry_combine, (1.0, 0.0, 0.0, 0.0), False)
    enter_re, enter_im = (chained[2], chained[3])
    positions = jnp.arange(seq_len, dtype=jnp.float32)
    ahead = positions + 1.0
    lift = jnp.exp(jnp.cumsum(log_keep)[:, None] - ahead[:, None] * log_rate[None, :])
    lift_re = lift * jnp.cos(ahead[:, None] * rotation[None, :])
    lift_im = lift * jnp.sin(ahead[:, None] * rotation[None, :])
    state_re = state_re + lift_re * enter_re[None, :] - lift_im * enter_im[None, :]
    state_im = state_im + lift_re * enter_im[None, :] + lift_im * enter_re[None, :]
    state_bf = jnp.concatenate(
        [
            state_re.reshape(seq_len, local_heads, state_size),
            state_im.reshape(seq_len, local_heads, state_size),
        ],
        axis=2,
    ).astype(jnp.bfloat16)
    mixed = jnp.einsum(
        "thk,hck->thc", state_bf, out_proj, preferred_element_type=jnp.float32
    ).reshape(seq_len, local_width)
    mixed = mixed + skip_gain * mixed_in.astype(jnp.float32)
    squares = jnp.sum(mixed * mixed, axis=1)
    scaled = cotangent.astype(jnp.float32) * norm_gain
    dots = jnp.sum(scaled * mixed, axis=1)
    squares, dots = jnp.sum(gather_all(jnp.stack([squares, dots]), "chan"), axis=0)
    model_width = local_width * lax.axis_size("chan")
    inverse = lax.rsqrt(squares / model_width + 1e-06)
    normed = (mixed * inverse[:, None] * norm_gain).astype(jnp.bfloat16)
    mixed_grad = inverse[:, None] * (
        scaled - mixed * (inverse * inverse * dots / model_width)[:, None]
    )
    grad_bf = mixed_grad.astype(jnp.bfloat16).reshape(seq_len, local_heads, head_width)
    state_grad = jnp.einsum("thc,hck->thk", grad_bf, out_proj, preferred_element_type=jnp.float32)
    out_grad = jnp.einsum("thc,thk->hck", grad_bf, state_bf, preferred_element_type=jnp.float32)
    back_keep = jnp.concatenate([jnp.zeros((1,), jnp.float32), log_keep[::-1][:-1]])
    grad_re = state_grad[:, :, :state_size].reshape(seq_len, num_cols)[::-1]
    grad_im = state_grad[:, :, state_size:].reshape(seq_len, num_cols)[::-1]
    adj_re, adj_im = linear_run(grad_re, grad_im, log_rate, -rotation, back_keep)
    first_mag = jnp.exp(log_keep[0] - log_rate)
    cos_turn = jnp.cos(rotation)
    sin_turn = jnp.sin(rotation)
    first_re = first_mag * (cos_turn * adj_re[-1] + sin_turn * adj_im[-1])
    first_im = first_mag * (cos_turn * adj_im[-1] - sin_turn * adj_re[-1])
    firsts = gather_all(jnp.stack([first_re, first_im]), SEQ)
    back_chained = carried_in(
        total_re, -total_im, firsts, SEQ, carry_combine, (1.0, 0.0, 0.0, 0.0), True
    )
    later_re, later_im = (back_chained[2], back_chained[3])
    back_lift = jnp.exp(jnp.cumsum(back_keep)[:, None] - positions[:, None] * log_rate[None, :])
    back_re = back_lift * jnp.cos(positions[:, None] * rotation[None, :])
    back_im = -back_lift * jnp.sin(positions[:, None] * rotation[None, :])
    adj_re = adj_re + back_re * later_re[None, :] - back_im * later_im[None, :]
    adj_im = adj_im + back_re * later_im[None, :] + back_im * later_re[None, :]
    adj_re = adj_re[::-1]
    adj_im = adj_im[::-1]
    drive_grad = jnp.concatenate(
        [
            (in_scale * adj_re).reshape(seq_len, local_heads, state_size),
            (in_scale * adj_im).reshape(seq_len, local_heads, state_size),
        ],
        axis=2,
    ).astype(jnp.bfloat16)
    in_grad = jnp.einsum("thc,thk->hck", by_head, drive_grad, preferred_element_type=jnp.float32)
    input_grad = jnp.einsum(
        "thk,hck->thc", drive_grad, in_proj, preferred_element_type=jnp.float32
    ).reshape(seq_len, local_width)
    input_grad = input_grad + skip_gain * mixed_grad
    trail_rows = from_behind(input_grad[: tap_count - 1], SEQ, -1)
    tail = jnp.concatenate([input_grad, trail_rows], axis=0)
    tokens_grad = conv_taps[0][None, :] * tail[:seq_len]
    for offset in range(1, tap_count):
        tokens_grad = tokens_grad + conv_taps[offset][None, :] * tail[offset : offset + seq_len]
    taps_grad = jnp.stack(
        [
            jnp.sum(
                input_grad * padded[tap_count - 1 - offset : tap_count - 1 - offset + seq_len],
                axis=0,
            )
            for offset in range(tap_count)
        ]
    )
    parts = (out_grad, in_grad, taps_grad)
    packed = tree_sum(jnp.concatenate([p.reshape(-1) for p in parts]), SEQ)
    ends = [0]
    for p in parts:
        ends.append(ends[-1] + p.size)
    out_grad, in_grad, taps_grad = (
        packed[a:b].reshape(p.shape) for a, b, p in zip(ends[:-1], ends[1:], parts)
    )
    return (normed, tokens_grad.astype(jnp.bfloat16), in_grad, out_grad, taps_grad)


def solution(mesh):
    seq_count, chan_count = mesh.devices.shape
    inner = 1
    while inner * inner < seq_count:
        inner *= 2
    devices = mesh.devices.reshape(seq_count // inner, inner, chan_count)
    mesh = Mesh(devices, SEQ + ("chan",))
    in_specs = (
        P(SEQ, "chan"),
        P(None, "chan"),
        P("chan"),
        P("chan"),
        P("chan", None, None),
        P("chan", None, None),
        P("chan"),
        P("chan"),
        P(SEQ),
        P(SEQ, "chan"),
    )
    out_specs = (
        P(SEQ, "chan"),
        P(SEQ, "chan"),
        P("chan", None, None),
        P("chan", None, None),
        P(None, "chan"),
    )
    return jax.shard_map(
        per_device, mesh=mesh, in_specs=in_specs, out_specs=out_specs, check_vma=False
    )
```

```python
import jax
import jax.numpy as jnp
from jax import lax
from jax.sharding import Mesh, PartitionSpec as P

SEQ = ("z", "y")


def from_behind(value, axis, by):
    length = lax.axis_size(axis)
    pairs = [(i, i + by) for i in range(length) if 0 <= i + by < length]
    return lax.ppermute(value, axis, pairs)


def tree_fold(stack, order, upto, combine, unit):
    count = len(order)
    width = count.bit_length() - 1
    flips = [int(format(r, f"0{width}b")[::-1], 2) for r in range(count)]
    level = jnp.take(stack, jnp.asarray([order[f] for f in flips]), axis=0)
    keep = jnp.asarray(flips)[:, None, None] < upto
    level = jnp.where(keep, level, unit[None])
    while level.shape[0] > 1:
        half = level.shape[0] // 2
        joined = combine(tuple(level[:half].swapaxes(0, 1)), tuple(level[half:].swapaxes(0, 1)))
        level = jnp.stack(joined, axis=1)
    return level[0]


def gather_all(value, axis):
    count = lax.axis_size(axis)
    spread = jnp.broadcast_to(value[None], (count,) + value.shape)
    return lax.all_to_all(spread, axis, 0, 0, tiled=True)


def carried_in(mult_re, mult_im, every, axis, combine, identity, reverse):
    every = jnp.concatenate([jnp.stack([mult_re, mult_im], axis=1), every[:, :2]], axis=1)
    unit = jnp.stack([jnp.zeros_like(mult_re[0]) + e for e in identity])
    place = lax.axis_index(axis)
    order = list(range(lax.axis_size(axis)))
    if reverse:
        order = order[::-1]
        place = lax.axis_size(axis) - 1 - place
    before = tree_fold(every, order, place, combine, unit)
    return tuple(before)


def tree_sum(value, axis):
    count = lax.axis_size(axis)
    flat = value.reshape(-1)
    width = -(-flat.size // count)
    block = jnp.pad(flat, (0, width * count - flat.size)).reshape(count, width)
    mine = jnp.sum(lax.all_to_all(block, axis, 0, 0, tiled=True), axis=0)
    return gather_all(mine, axis).reshape(-1)[: flat.size].reshape(value.shape)


def linear_run(drive_re, drive_im, decay_rate, turn_rate, log_keep):
    seq_len, num_cols = drive_re.shape
    block_len = min(64, seq_len)
    block_count = seq_len // block_len
    offsets = jnp.arange(block_len, dtype=jnp.float32)
    keep_cum = jnp.cumsum(log_keep.reshape(block_count, block_len), axis=1)[:, :, None]
    angles = offsets[:, None] * turn_rate[None, :]
    cosine = jnp.cos(angles)
    sine = jnp.sin(angles)
    growth = jnp.exp(offsets[None, :, None] * decay_rate[None, None, :] - keep_cum)
    blk_re = drive_re.reshape(block_count, block_len, num_cols)
    blk_im = drive_im.reshape(block_count, block_len, num_cols)
    pre_re = growth * (blk_re * cosine + blk_im * sine)
    pre_im = growth * (blk_im * cosine - blk_re * sine)
    lower_ones = (offsets[:, None] >= offsets[None, :]).astype(jnp.float32)
    summed = jnp.einsum(
        "ji,abik->abjk", lower_ones, jnp.stack([pre_re, pre_im]), precision=lax.Precision.HIGHEST
    )
    shrink = jnp.exp(keep_cum - offsets[None, :, None] * decay_rate[None, None, :])
    state_re = shrink * (summed[0] * cosine - summed[1] * sine)
    state_im = shrink * (summed[0] * sine + summed[1] * cosine)
    step_mag = jnp.exp(keep_cum[:, -1] - block_len * decay_rate[None, :])
    step_re = step_mag * jnp.cos(block_len * turn_rate)[None, :]
    step_im = step_mag * jnp.sin(block_len * turn_rate)[None, :]

    def advance(carried, inputs):
        carry_re, carry_im = carried
        mult_re, mult_im, end_re, end_im = inputs
        next_re = mult_re * carry_re - mult_im * carry_im + end_re
        next_im = mult_re * carry_im + mult_im * carry_re + end_im
        return ((next_re, next_im), (carry_re, carry_im))

    zeros_col = jnp.zeros((num_cols,), jnp.float32)
    enter_re, enter_im = lax.scan(
        advance, (zeros_col, zeros_col), (step_re, step_im, state_re[:, -1], state_im[:, -1])
    )[1]
    ahead = offsets + 1.0
    lift = jnp.exp(keep_cum - ahead[None, :, None] * decay_rate[None, None, :])
    lift_re = lift * jnp.cos(ahead[:, None] * turn_rate[None, :])
    lift_im = lift * jnp.sin(ahead[:, None] * turn_rate[None, :])
    state_re = state_re + lift_re * enter_re[:, None] - lift_im * enter_im[:, None]
    state_im = state_im + lift_re * enter_im[:, None] + lift_im * enter_re[:, None]
    return (state_re.reshape(seq_len, num_cols), state_im.reshape(seq_len, num_cols))


def carry_combine(earlier, later):
    early_re, early_im, early_sre, early_sim = earlier
    late_re, late_im, late_sre, late_sim = later
    joined_re = early_re * late_re - early_im * late_im
    joined_im = early_re * late_im + early_im * late_re
    joined_sre = late_re * early_sre - late_im * early_sim + late_sre
    joined_sim = late_re * early_sim + late_im * early_sre + late_sim
    return (joined_re, joined_im, joined_sre, joined_sim)


def per_device(
    tokens,
    conv_taps,
    log_rate,
    rotation,
    in_proj,
    out_proj,
    skip_gain,
    norm_gain,
    retention,
    cotangent,
):
    seq_len, local_width = tokens.shape
    tap_count = conv_taps.shape[0]
    local_heads, head_width, double_state = in_proj.shape
    state_size = double_state // 2
    num_cols = local_heads * state_size
    lead_rows = from_behind(tokens[seq_len - (tap_count - 1) :], SEQ, 1)
    padded = jnp.concatenate([lead_rows, tokens], axis=0).astype(jnp.float32)
    conv_sum = conv_taps[0][None, :] * padded[tap_count - 1 :]
    for offset in range(1, tap_count):
        conv_sum = (
            conv_sum
            + conv_taps[offset][None, :]
            * padded[tap_count - 1 - offset : tap_count - 1 - offset + seq_len]
        )
    mixed_in = conv_sum.astype(jnp.bfloat16)
    by_head = mixed_in.reshape(seq_len, local_heads, head_width)
    projected = jnp.einsum("thc,hck->thk", by_head, in_proj, preferred_element_type=jnp.float32)
    in_scale = jnp.sqrt(-jnp.expm1(-2.0 * log_rate))
    drive_re = projected[:, :, :state_size].reshape(seq_len, num_cols) * in_scale
    drive_im = projected[:, :, state_size:].reshape(seq_len, num_cols) * in_scale
    log_keep = jnp.log(retention)
    state_re, state_im = linear_run(drive_re, drive_im, log_rate, rotation, log_keep)
    keep_total = jnp.sum(log_keep)
    ends = gather_all(
        jnp.stack([state_re[-1], state_im[-1], jnp.broadcast_to(keep_total, state_re[-1].shape)]), SEQ
    )
    total_mag = jnp.exp(ends[:, 2, :1] - seq_len * log_rate)
    total_re = total_mag * jnp.cos(seq_len * rotation)
    total_im = total_mag * jnp.sin(seq_len * rotation)
    chained = carried_in(total_re, total_im, ends, SEQ, carry_combine, (1.0, 0.0, 0.0, 0.0), False)
    enter_re, enter_im = (chained[2], chained[3])
    positions = jnp.arange(seq_len, dtype=jnp.float32)
    ahead = positions + 1.0
    lift = jnp.exp(jnp.cumsum(log_keep)[:, None] - ahead[:, None] * log_rate[None, :])
    lift_re = lift * jnp.cos(ahead[:, None] * rotation[None, :])
    lift_im = lift * jnp.sin(ahead[:, None] * rotation[None, :])
    state_re = state_re + lift_re * enter_re[None, :] - lift_im * enter_im[None, :]
    state_im = state_im + lift_re * enter_im[None, :] + lift_im * enter_re[None, :]
    state_bf = jnp.concatenate(
        [
            state_re.reshape(seq_len, local_heads, state_size),
            state_im.reshape(seq_len, local_heads, state_size),
        ],
        axis=2,
    ).astype(jnp.bfloat16)
    state_bf = lax.optimization_barrier(state_bf)
    mixed = jnp.einsum(
        "thk,hck->thc", state_bf, out_proj, preferred_element_type=jnp.float32
    ).reshape(seq_len, local_width)
    mixed = mixed + skip_gain * mixed_in.astype(jnp.float32)
    squares = jnp.sum(mixed * mixed, axis=1)
    scaled = cotangent.astype(jnp.float32) * norm_gain
    dots = jnp.sum(scaled * mixed, axis=1)
    squares, dots = jnp.sum(gather_all(jnp.stack([squares, dots]), "chan"), axis=0)
    model_width = local_width * lax.axis_size("chan")
    inverse = lax.rsqrt(squares / model_width + 1e-06)
    normed = (mixed * inverse[:, None] * norm_gain).astype(jnp.bfloat16)
    mixed_grad = inverse[:, None] * (
        scaled - mixed * (inverse * inverse * dots / model_width)[:, None]
    )
    grad_bf = mixed_grad.astype(jnp.bfloat16).reshape(seq_len, local_heads, head_width)
    state_grad = jnp.einsum("thc,hck->thk", grad_bf, out_proj, preferred_element_type=jnp.float32)
    out_grad = jnp.einsum("thc,thk->hck", grad_bf, state_bf, preferred_element_type=jnp.float32)
    back_keep = jnp.concatenate([jnp.zeros((1,), jnp.float32), log_keep[::-1][:-1]])
    grad_re = state_grad[:, :, :state_size].reshape(seq_len, num_cols)[::-1]
    grad_im = state_grad[:, :, state_size:].reshape(seq_len, num_cols)[::-1]
    adj_re, adj_im = linear_run(grad_re, grad_im, log_rate, -rotation, back_keep)
    first_mag = jnp.exp(log_keep[0] - log_rate)
    cos_turn = jnp.cos(rotation)
    sin_turn = jnp.sin(rotation)
    first_re = first_mag * (cos_turn * adj_re[-1] + sin_turn * adj_im[-1])
    first_im = first_mag * (cos_turn * adj_im[-1] - sin_turn * adj_re[-1])
    firsts = gather_all(jnp.stack([first_re, first_im]), SEQ)
    back_chained = carried_in(
        total_re, -total_im, firsts, SEQ, carry_combine, (1.0, 0.0, 0.0, 0.0), True
    )
    later_re, later_im = (back_chained[2], back_chained[3])
    back_lift = jnp.exp(jnp.cumsum(back_keep)[:, None] - positions[:, None] * log_rate[None, :])
    back_re = back_lift * jnp.cos(positions[:, None] * rotation[None, :])
    back_im = -back_lift * jnp.sin(positions[:, None] * rotation[None, :])
    adj_re = adj_re + back_re * later_re[None, :] - back_im * later_im[None, :]
    adj_im = adj_im + back_re * later_im[None, :] + back_im * later_re[None, :]
    adj_re = adj_re[::-1]
    adj_im = adj_im[::-1]
    drive_grad = jnp.concatenate(
        [
            (in_scale * adj_re).reshape(seq_len, local_heads, state_size),
            (in_scale * adj_im).reshape(seq_len, local_heads, state_size),
        ],
        axis=2,
    ).astype(jnp.bfloat16)
    drive_grad = lax.optimization_barrier(drive_grad)
    in_grad = jnp.einsum("thc,thk->hck", by_head, drive_grad, preferred_element_type=jnp.float32)
    input_grad = jnp.einsum(
        "thk,hck->thc", drive_grad, in_proj, preferred_element_type=jnp.float32
    ).reshape(seq_len, local_width)
    input_grad = input_grad + skip_gain * mixed_grad
    trail_rows = from_behind(input_grad[: tap_count - 1], SEQ, -1)
    tail = jnp.concatenate([input_grad, trail_rows], axis=0)
    tokens_grad = conv_taps[0][None, :] * tail[:seq_len]
    for offset in range(1, tap_count):
        tokens_grad = tokens_grad + conv_taps[offset][None, :] * tail[offset : offset + seq_len]
    taps_grad = jnp.stack(
        [
            jnp.sum(
                input_grad * padded[tap_count - 1 - offset : tap_count - 1 - offset + seq_len],
                axis=0,
            )
            for offset in range(tap_count)
        ]
    )
    parts = (out_grad, in_grad, taps_grad)
    packed = tree_sum(jnp.concatenate([p.reshape(-1) for p in parts]), SEQ)
    ends = [0]
    for p in parts:
        ends.append(ends[-1] + p.size)
    out_grad, in_grad, taps_grad = (
        packed[a:b].reshape(p.shape) for a, b, p in zip(ends[:-1], ends[1:], parts)
    )
    return (normed, tokens_grad.astype(jnp.bfloat16), in_grad, out_grad, taps_grad)


def solution(mesh):
    seq_count, chan_count = mesh.devices.shape
    inner = 1
    while inner * inner < seq_count:
        inner *= 2
    devices = mesh.devices.reshape(seq_count // inner, inner, chan_count)
    mesh = Mesh(devices, SEQ + ("chan",))
    in_specs = (
        P(SEQ, "chan"),
        P(None, "chan"),
        P("chan"),
        P("chan"),
        P("chan", None, None),
        P("chan", None, None),
        P("chan"),
        P("chan"),
        P(SEQ),
        P(SEQ, "chan"),
    )
    out_specs = (
        P(SEQ, "chan"),
        P(SEQ, "chan"),
        P("chan", None, None),
        P("chan", None, None),
        P(None, "chan"),
    )
    return jax.shard_map(
        per_device, mesh=mesh, in_specs=in_specs, out_specs=out_specs, check_vma=False
    )
```

```python
import jax
import jax.numpy as jnp
from jax import lax
from jax.sharding import Mesh, PartitionSpec as P

SEQ = ("z", "y")


def from_behind(value, axis, by):
    length = lax.axis_size(axis)
    pairs = [(i, i + by) for i in range(length) if 0 <= i + by < length]
    return lax.ppermute(value, axis, pairs)


def tree_fold(stack, order, upto, combine, unit):
    count = len(order)
    width = count.bit_length() - 1
    flips = [int(format(r, f"0{width}b")[::-1], 2) for r in range(count)]
    level = jnp.take(stack, jnp.asarray([order[f] for f in flips]), axis=0)
    keep = jnp.asarray(flips)[:, None, None] < upto
    level = jnp.where(keep, level, unit[None])
    while level.shape[0] > 1:
        half = level.shape[0] // 2
        joined = combine(tuple(level[:half].swapaxes(0, 1)), tuple(level[half:].swapaxes(0, 1)))
        level = jnp.stack(joined, axis=1)
    return level[0]


def gather_all(value, axis):
    count = lax.axis_size(axis)
    spread = jnp.broadcast_to(value[None], (count,) + value.shape)
    return lax.all_to_all(spread, axis, 0, 0, tiled=True)


def fold(stack, where_at, combine, unit):
    total = unit
    prefix = unit
    for j in range(stack.shape[0]):
        prefix = jnp.where(j == where_at, total, prefix)
        total = jnp.stack(combine(tuple(total), tuple(stack[j])))
    return prefix, total


def carried_in(part, axis, combine, identity, reverse):
    outer, inner = axis
    packed = jnp.stack(part)
    unit = jnp.stack([jnp.zeros_like(part[0]) + e for e in identity])
    row_place = lax.axis_index(inner)
    col_place = lax.axis_index(outer)
    row = gather_all(packed, inner)
    if reverse:
        row = row[::-1]
        row_place = lax.axis_size(inner) - 1 - row_place
        col_place = lax.axis_size(outer) - 1 - col_place
    within, row_total = fold(row, row_place, combine, unit)
    rows = gather_all(row_total, outer)
    if reverse:
        rows = rows[::-1]
    before, _ = fold(rows, col_place, combine, unit)
    return combine(tuple(before), tuple(within))


def tree_sum(value, axis):
    count = lax.axis_size(axis)
    flat = value.reshape(-1)
    width = -(-flat.size // count)
    block = jnp.pad(flat, (0, width * count - flat.size)).reshape(count, width)
    mine = jnp.sum(lax.all_to_all(block, axis, 0, 0, tiled=True), axis=0)
    return gather_all(mine, axis).reshape(-1)[: flat.size].reshape(value.shape)


def linear_run(drive_re, drive_im, decay_rate, turn_rate, log_keep):
    seq_len, num_cols = drive_re.shape
    block_len = min(64, seq_len)
    block_count = seq_len // block_len
    offsets = jnp.arange(block_len, dtype=jnp.float32)
    keep_cum = jnp.cumsum(log_keep.reshape(block_count, block_len), axis=1)[:, :, None]
    angles = offsets[:, None] * turn_rate[None, :]
    cosine = jnp.cos(angles)
    sine = jnp.sin(angles)
    growth = jnp.exp(offsets[None, :, None] * decay_rate[None, None, :] - keep_cum)
    blk_re = drive_re.reshape(block_count, block_len, num_cols)
    blk_im = drive_im.reshape(block_count, block_len, num_cols)
    pre_re = growth * (blk_re * cosine + blk_im * sine)
    pre_im = growth * (blk_im * cosine - blk_re * sine)
    lower_ones = (offsets[:, None] >= offsets[None, :]).astype(jnp.float32)
    summed = jnp.einsum(
        "ji,abik->abjk", lower_ones, jnp.stack([pre_re, pre_im]), precision=lax.Precision.HIGHEST
    )
    shrink = jnp.exp(keep_cum - offsets[None, :, None] * decay_rate[None, None, :])
    state_re = shrink * (summed[0] * cosine - summed[1] * sine)
    state_im = shrink * (summed[0] * sine + summed[1] * cosine)
    step_mag = jnp.exp(keep_cum[:, -1] - block_len * decay_rate[None, :])
    step_re = step_mag * jnp.cos(block_len * turn_rate)[None, :]
    step_im = step_mag * jnp.sin(block_len * turn_rate)[None, :]

    def advance(carried, inputs):
        carry_re, carry_im = carried
        mult_re, mult_im, end_re, end_im = inputs
        next_re = mult_re * carry_re - mult_im * carry_im + end_re
        next_im = mult_re * carry_im + mult_im * carry_re + end_im
        return ((next_re, next_im), (carry_re, carry_im))

    zeros_col = jnp.zeros((num_cols,), jnp.float32)
    enter_re, enter_im = lax.scan(
        advance, (zeros_col, zeros_col), (step_re, step_im, state_re[:, -1], state_im[:, -1])
    )[1]
    ahead = offsets + 1.0
    lift = jnp.exp(keep_cum - ahead[None, :, None] * decay_rate[None, None, :])
    lift_re = lift * jnp.cos(ahead[:, None] * turn_rate[None, :])
    lift_im = lift * jnp.sin(ahead[:, None] * turn_rate[None, :])
    state_re = state_re + lift_re * enter_re[:, None] - lift_im * enter_im[:, None]
    state_im = state_im + lift_re * enter_im[:, None] + lift_im * enter_re[:, None]
    return (state_re.reshape(seq_len, num_cols), state_im.reshape(seq_len, num_cols))


def carry_combine(earlier, later):
    early_re, early_im, early_sre, early_sim = earlier
    late_re, late_im, late_sre, late_sim = later
    joined_re = early_re * late_re - early_im * late_im
    joined_im = early_re * late_im + early_im * late_re
    joined_sre = late_re * early_sre - late_im * early_sim + late_sre
    joined_sim = late_re * early_sim + late_im * early_sre + late_sim
    return (joined_re, joined_im, joined_sre, joined_sim)


def per_device(
    tokens,
    conv_taps,
    log_rate,
    rotation,
    in_proj,
    out_proj,
    skip_gain,
    norm_gain,
    retention,
    cotangent,
):
    seq_len, local_width = tokens.shape
    tap_count = conv_taps.shape[0]
    local_heads, head_width, double_state = in_proj.shape
    state_size = double_state // 2
    num_cols = local_heads * state_size
    lead_rows = from_behind(tokens[seq_len - (tap_count - 1) :], SEQ, 1)
    padded = jnp.concatenate([lead_rows, tokens], axis=0).astype(jnp.float32)
    conv_sum = conv_taps[0][None, :] * padded[tap_count - 1 :]
    for offset in range(1, tap_count):
        conv_sum = (
            conv_sum
            + conv_taps[offset][None, :]
            * padded[tap_count - 1 - offset : tap_count - 1 - offset + seq_len]
        )
    mixed_in = conv_sum.astype(jnp.bfloat16)
    by_head = mixed_in.reshape(seq_len, local_heads, head_width)
    projected = jnp.einsum("thc,hck->thk", by_head, in_proj, preferred_element_type=jnp.float32)
    in_scale = jnp.sqrt(-jnp.expm1(-2.0 * log_rate))
    drive_re = projected[:, :, :state_size].reshape(seq_len, num_cols) * in_scale
    drive_im = projected[:, :, state_size:].reshape(seq_len, num_cols) * in_scale
    log_keep = jnp.log(retention)
    state_re, state_im = linear_run(drive_re, drive_im, log_rate, rotation, log_keep)
    keep_total = jnp.sum(log_keep)
    total_mag = jnp.exp(keep_total - seq_len * log_rate)
    total_re = total_mag * jnp.cos(seq_len * rotation)
    total_im = total_mag * jnp.sin(seq_len * rotation)
    chained = carried_in(
        (total_re, total_im, state_re[-1], state_im[-1]), SEQ, carry_combine, (1.0, 0.0, 0.0, 0.0), False
    )
    enter_re, enter_im = (chained[2], chained[3])
    positions = jnp.arange(seq_len, dtype=jnp.float32)
    ahead = positions + 1.0
    lift = jnp.exp(jnp.cumsum(log_keep)[:, None] - ahead[:, None] * log_rate[None, :])
    lift_re = lift * jnp.cos(ahead[:, None] * rotation[None, :])
    lift_im = lift * jnp.sin(ahead[:, None] * rotation[None, :])
    state_re = state_re + lift_re * enter_re[None, :] - lift_im * enter_im[None, :]
    state_im = state_im + lift_re * enter_im[None, :] + lift_im * enter_re[None, :]
    state_bf = jnp.concatenate(
        [
            state_re.reshape(seq_len, local_heads, state_size),
            state_im.reshape(seq_len, local_heads, state_size),
        ],
        axis=2,
    ).astype(jnp.bfloat16)
    mixed = jnp.einsum(
        "thk,hck->thc", state_bf, out_proj, preferred_element_type=jnp.float32
    ).reshape(seq_len, local_width)
    mixed = mixed + skip_gain * mixed_in.astype(jnp.float32)
    squares = jnp.sum(mixed * mixed, axis=1)
    scaled = cotangent.astype(jnp.float32) * norm_gain
    dots = jnp.sum(scaled * mixed, axis=1)
    squares, dots = jnp.sum(gather_all(jnp.stack([squares, dots]), "chan"), axis=0)
    model_width = local_width * lax.axis_size("chan")
    inverse = lax.rsqrt(squares / model_width + 1e-06)
    normed = (mixed * inverse[:, None] * norm_gain).astype(jnp.bfloat16)
    mixed_grad = inverse[:, None] * (
        scaled - mixed * (inverse * inverse * dots / model_width)[:, None]
    )
    grad_bf = mixed_grad.astype(jnp.bfloat16).reshape(seq_len, local_heads, head_width)
    state_grad = jnp.einsum("thc,hck->thk", grad_bf, out_proj, preferred_element_type=jnp.float32)
    out_grad = jnp.einsum("thc,thk->hck", grad_bf, state_bf, preferred_element_type=jnp.float32)
    back_keep = jnp.concatenate([jnp.zeros((1,), jnp.float32), log_keep[::-1][:-1]])
    grad_re = state_grad[:, :, :state_size].reshape(seq_len, num_cols)[::-1]
    grad_im = state_grad[:, :, state_size:].reshape(seq_len, num_cols)[::-1]
    adj_re, adj_im = linear_run(grad_re, grad_im, log_rate, -rotation, back_keep)
    first_mag = jnp.exp(log_keep[0] - log_rate)
    cos_turn = jnp.cos(rotation)
    sin_turn = jnp.sin(rotation)
    first_re = first_mag * (cos_turn * adj_re[-1] + sin_turn * adj_im[-1])
    first_im = first_mag * (cos_turn * adj_im[-1] - sin_turn * adj_re[-1])
    back_chained = carried_in(
        (total_re, -total_im, first_re, first_im), SEQ, carry_combine, (1.0, 0.0, 0.0, 0.0), True
    )
    later_re, later_im = (back_chained[2], back_chained[3])
    back_lift = jnp.exp(jnp.cumsum(back_keep)[:, None] - positions[:, None] * log_rate[None, :])
    back_re = back_lift * jnp.cos(positions[:, None] * rotation[None, :])
    back_im = -back_lift * jnp.sin(positions[:, None] * rotation[None, :])
    adj_re = adj_re + back_re * later_re[None, :] - back_im * later_im[None, :]
    adj_im = adj_im + back_re * later_im[None, :] + back_im * later_re[None, :]
    adj_re = adj_re[::-1]
    adj_im = adj_im[::-1]
    drive_grad = jnp.concatenate(
        [
            (in_scale * adj_re).reshape(seq_len, local_heads, state_size),
            (in_scale * adj_im).reshape(seq_len, local_heads, state_size),
        ],
        axis=2,
    ).astype(jnp.bfloat16)
    in_grad = jnp.einsum("thc,thk->hck", by_head, drive_grad, preferred_element_type=jnp.float32)
    input_grad = jnp.einsum(
        "thk,hck->thc", drive_grad, in_proj, preferred_element_type=jnp.float32
    ).reshape(seq_len, local_width)
    input_grad = input_grad + skip_gain * mixed_grad
    trail_rows = from_behind(input_grad[: tap_count - 1], SEQ, -1)
    tail = jnp.concatenate([input_grad, trail_rows], axis=0)
    tokens_grad = conv_taps[0][None, :] * tail[:seq_len]
    for offset in range(1, tap_count):
        tokens_grad = tokens_grad + conv_taps[offset][None, :] * tail[offset : offset + seq_len]
    taps_grad = jnp.stack(
        [
            jnp.sum(
                input_grad * padded[tap_count - 1 - offset : tap_count - 1 - offset + seq_len],
                axis=0,
            )
            for offset in range(tap_count)
        ]
    )
    parts = (out_grad, in_grad, taps_grad)
    packed = tree_sum(jnp.concatenate([p.reshape(-1) for p in parts]), SEQ)
    ends = [0]
    for p in parts:
        ends.append(ends[-1] + p.size)
    out_grad, in_grad, taps_grad = (
        packed[a:b].reshape(p.shape) for a, b, p in zip(ends[:-1], ends[1:], parts)
    )
    return (normed, tokens_grad.astype(jnp.bfloat16), in_grad, out_grad, taps_grad)


def solution(mesh):
    seq_count, chan_count = mesh.devices.shape
    inner = 1
    while inner * inner < seq_count:
        inner *= 2
    devices = mesh.devices.reshape(seq_count // inner, inner, chan_count)
    mesh = Mesh(devices, SEQ + ("chan",))
    in_specs = (
        P(SEQ, "chan"),
        P(None, "chan"),
        P("chan"),
        P("chan"),
        P("chan", None, None),
        P("chan", None, None),
        P("chan"),
        P("chan"),
        P(SEQ),
        P(SEQ, "chan"),
    )
    out_specs = (
        P(SEQ, "chan"),
        P(SEQ, "chan"),
        P("chan", None, None),
        P("chan", None, None),
        P(None, "chan"),
    )
    return jax.shard_map(
        per_device, mesh=mesh, in_specs=in_specs, out_specs=out_specs, check_vma=False
    )
```

```python
import jax
import jax.numpy as jnp
from jax import lax
from jax.sharding import Mesh, PartitionSpec as P

SEQ = ("z", "y")


def from_behind(value, axis, by):
    length = lax.axis_size(axis)
    pairs = [(i, i + by) for i in range(length) if 0 <= i + by < length]
    return lax.ppermute(value, axis, pairs)


def tree_fold(stack, order, upto, combine, unit):
    count = len(order)
    width = count.bit_length() - 1
    flips = [int(format(r, f"0{width}b")[::-1], 2) for r in range(count)]
    level = jnp.take(stack, jnp.asarray([order[f] for f in flips]), axis=0)
    keep = jnp.asarray(flips)[:, None, None] < upto
    level = jnp.where(keep, level, unit[None])
    while level.shape[0] > 1:
        half = level.shape[0] // 2
        joined = combine(tuple(level[:half].swapaxes(0, 1)), tuple(level[half:].swapaxes(0, 1)))
        level = jnp.stack(joined, axis=1)
    return level[0]


def gather_all(value, axis):
    count = lax.axis_size(axis)
    spread = jnp.broadcast_to(value[None], (count,) + value.shape)
    return lax.all_to_all(spread, axis, 0, 0, tiled=True)


def fold(stack, where_at, combine, unit):
    total = unit
    prefix = unit
    for j in range(stack.shape[0]):
        prefix = jnp.where(j == where_at, total, prefix)
        total = jnp.stack(combine(tuple(total), tuple(stack[j])))
    return prefix, total


def carried_in(part, axis, combine, identity, reverse):
    outer, inner = axis
    packed = jnp.stack(part)
    unit = jnp.stack([jnp.zeros_like(part[0]) + e for e in identity])
    row_place = lax.axis_index(inner)
    col_place = lax.axis_index(outer)
    row = gather_all(packed, inner)
    if reverse:
        row = row[::-1]
        row_place = lax.axis_size(inner) - 1 - row_place
        col_place = lax.axis_size(outer) - 1 - col_place
    within, row_total = fold(row, row_place, combine, unit)
    rows = gather_all(row_total, outer)
    if reverse:
        rows = rows[::-1]
    before, _ = fold(rows, col_place, combine, unit)
    return combine(tuple(before), tuple(within))


def tree_sum(value, axis):
    flat = value.reshape(-1)
    count = 1
    for name in axis:
        count *= lax.axis_size(name)
    width = -(-flat.size // count)
    block = jnp.pad(flat, (0, width * count - flat.size))
    for name in axis[::-1]:
        block = block.reshape(lax.axis_size(name), -1)
        block = jnp.sum(lax.all_to_all(block, name, 0, 0, tiled=True), axis=0)
    for name in axis:
        block = gather_all(block, name).reshape(-1)
    return block[: flat.size].reshape(value.shape)


def linear_run(drive_re, drive_im, decay_rate, turn_rate, log_keep):
    seq_len, num_cols = drive_re.shape
    block_len = min(64, seq_len)
    block_count = seq_len // block_len
    offsets = jnp.arange(block_len, dtype=jnp.float32)
    keep_cum = jnp.cumsum(log_keep.reshape(block_count, block_len), axis=1)[:, :, None]
    angles = offsets[:, None] * turn_rate[None, :]
    cosine = jnp.cos(angles)
    sine = jnp.sin(angles)
    growth = jnp.exp(offsets[None, :, None] * decay_rate[None, None, :] - keep_cum)
    blk_re = drive_re.reshape(block_count, block_len, num_cols)
    blk_im = drive_im.reshape(block_count, block_len, num_cols)
    pre_re = growth * (blk_re * cosine + blk_im * sine)
    pre_im = growth * (blk_im * cosine - blk_re * sine)
    lower_ones = (offsets[:, None] >= offsets[None, :]).astype(jnp.float32)
    summed = jnp.einsum(
        "ji,abik->abjk", lower_ones, jnp.stack([pre_re, pre_im]), precision=lax.Precision.HIGHEST
    )
    shrink = jnp.exp(keep_cum - offsets[None, :, None] * decay_rate[None, None, :])
    state_re = shrink * (summed[0] * cosine - summed[1] * sine)
    state_im = shrink * (summed[0] * sine + summed[1] * cosine)
    step_mag = jnp.exp(keep_cum[:, -1] - block_len * decay_rate[None, :])
    step_re = step_mag * jnp.cos(block_len * turn_rate)[None, :]
    step_im = step_mag * jnp.sin(block_len * turn_rate)[None, :]

    def advance(carried, inputs):
        carry_re, carry_im = carried
        mult_re, mult_im, end_re, end_im = inputs
        next_re = mult_re * carry_re - mult_im * carry_im + end_re
        next_im = mult_re * carry_im + mult_im * carry_re + end_im
        return ((next_re, next_im), (carry_re, carry_im))

    zeros_col = jnp.zeros((num_cols,), jnp.float32)
    enter_re, enter_im = lax.scan(
        advance, (zeros_col, zeros_col), (step_re, step_im, state_re[:, -1], state_im[:, -1])
    )[1]
    ahead = offsets + 1.0
    lift = jnp.exp(keep_cum - ahead[None, :, None] * decay_rate[None, None, :])
    lift_re = lift * jnp.cos(ahead[:, None] * turn_rate[None, :])
    lift_im = lift * jnp.sin(ahead[:, None] * turn_rate[None, :])
    state_re = state_re + lift_re * enter_re[:, None] - lift_im * enter_im[:, None]
    state_im = state_im + lift_re * enter_im[:, None] + lift_im * enter_re[:, None]
    return (state_re.reshape(seq_len, num_cols), state_im.reshape(seq_len, num_cols))


def carry_combine(earlier, later):
    early_re, early_im, early_sre, early_sim = earlier
    late_re, late_im, late_sre, late_sim = later
    joined_re = early_re * late_re - early_im * late_im
    joined_im = early_re * late_im + early_im * late_re
    joined_sre = late_re * early_sre - late_im * early_sim + late_sre
    joined_sim = late_re * early_sim + late_im * early_sre + late_sim
    return (joined_re, joined_im, joined_sre, joined_sim)


def per_device(
    tokens,
    conv_taps,
    log_rate,
    rotation,
    in_proj,
    out_proj,
    skip_gain,
    norm_gain,
    retention,
    cotangent,
):
    seq_len, local_width = tokens.shape
    tap_count = conv_taps.shape[0]
    local_heads, head_width, double_state = in_proj.shape
    state_size = double_state // 2
    num_cols = local_heads * state_size
    lead_rows = from_behind(tokens[seq_len - (tap_count - 1) :], SEQ, 1)
    padded = jnp.concatenate([lead_rows, tokens], axis=0).astype(jnp.float32)
    conv_sum = conv_taps[0][None, :] * padded[tap_count - 1 :]
    for offset in range(1, tap_count):
        conv_sum = (
            conv_sum
            + conv_taps[offset][None, :]
            * padded[tap_count - 1 - offset : tap_count - 1 - offset + seq_len]
        )
    mixed_in = conv_sum.astype(jnp.bfloat16)
    by_head = mixed_in.reshape(seq_len, local_heads, head_width)
    projected = jnp.einsum("thc,hck->thk", by_head, in_proj, preferred_element_type=jnp.float32)
    in_scale = jnp.sqrt(-jnp.expm1(-2.0 * log_rate))
    drive_re = projected[:, :, :state_size].reshape(seq_len, num_cols) * in_scale
    drive_im = projected[:, :, state_size:].reshape(seq_len, num_cols) * in_scale
    log_keep = jnp.log(retention)
    state_re, state_im = linear_run(drive_re, drive_im, log_rate, rotation, log_keep)
    keep_total = jnp.sum(log_keep)
    total_mag = jnp.exp(keep_total - seq_len * log_rate)
    total_re = total_mag * jnp.cos(seq_len * rotation)
    total_im = total_mag * jnp.sin(seq_len * rotation)
    chained = carried_in(
        (total_re, total_im, state_re[-1], state_im[-1]), SEQ, carry_combine, (1.0, 0.0, 0.0, 0.0), False
    )
    enter_re, enter_im = (chained[2], chained[3])
    positions = jnp.arange(seq_len, dtype=jnp.float32)
    ahead = positions + 1.0
    lift = jnp.exp(jnp.cumsum(log_keep)[:, None] - ahead[:, None] * log_rate[None, :])
    lift_re = lift * jnp.cos(ahead[:, None] * rotation[None, :])
    lift_im = lift * jnp.sin(ahead[:, None] * rotation[None, :])
    state_re = state_re + lift_re * enter_re[None, :] - lift_im * enter_im[None, :]
    state_im = state_im + lift_re * enter_im[None, :] + lift_im * enter_re[None, :]
    state_bf = jnp.concatenate(
        [
            state_re.reshape(seq_len, local_heads, state_size),
            state_im.reshape(seq_len, local_heads, state_size),
        ],
        axis=2,
    ).astype(jnp.bfloat16)
    mixed = jnp.einsum(
        "thk,hck->thc", state_bf, out_proj, preferred_element_type=jnp.float32
    ).reshape(seq_len, local_width)
    mixed = mixed + skip_gain * mixed_in.astype(jnp.float32)
    squares = jnp.sum(mixed * mixed, axis=1)
    scaled = cotangent.astype(jnp.float32) * norm_gain
    dots = jnp.sum(scaled * mixed, axis=1)
    squares, dots = jnp.sum(gather_all(jnp.stack([squares, dots]), "chan"), axis=0)
    model_width = local_width * lax.axis_size("chan")
    inverse = lax.rsqrt(squares / model_width + 1e-06)
    normed = (mixed * inverse[:, None] * norm_gain).astype(jnp.bfloat16)
    mixed_grad = inverse[:, None] * (
        scaled - mixed * (inverse * inverse * dots / model_width)[:, None]
    )
    grad_bf = mixed_grad.astype(jnp.bfloat16).reshape(seq_len, local_heads, head_width)
    state_grad = jnp.einsum("thc,hck->thk", grad_bf, out_proj, preferred_element_type=jnp.float32)
    out_grad = jnp.einsum("thc,thk->hck", grad_bf, state_bf, preferred_element_type=jnp.float32)
    back_keep = jnp.concatenate([jnp.zeros((1,), jnp.float32), log_keep[::-1][:-1]])
    grad_re = state_grad[:, :, :state_size].reshape(seq_len, num_cols)[::-1]
    grad_im = state_grad[:, :, state_size:].reshape(seq_len, num_cols)[::-1]
    adj_re, adj_im = linear_run(grad_re, grad_im, log_rate, -rotation, back_keep)
    first_mag = jnp.exp(log_keep[0] - log_rate)
    cos_turn = jnp.cos(rotation)
    sin_turn = jnp.sin(rotation)
    first_re = first_mag * (cos_turn * adj_re[-1] + sin_turn * adj_im[-1])
    first_im = first_mag * (cos_turn * adj_im[-1] - sin_turn * adj_re[-1])
    back_chained = carried_in(
        (total_re, -total_im, first_re, first_im), SEQ, carry_combine, (1.0, 0.0, 0.0, 0.0), True
    )
    later_re, later_im = (back_chained[2], back_chained[3])
    back_lift = jnp.exp(jnp.cumsum(back_keep)[:, None] - positions[:, None] * log_rate[None, :])
    back_re = back_lift * jnp.cos(positions[:, None] * rotation[None, :])
    back_im = -back_lift * jnp.sin(positions[:, None] * rotation[None, :])
    adj_re = adj_re + back_re * later_re[None, :] - back_im * later_im[None, :]
    adj_im = adj_im + back_re * later_im[None, :] + back_im * later_re[None, :]
    adj_re = adj_re[::-1]
    adj_im = adj_im[::-1]
    drive_grad = jnp.concatenate(
        [
            (in_scale * adj_re).reshape(seq_len, local_heads, state_size),
            (in_scale * adj_im).reshape(seq_len, local_heads, state_size),
        ],
        axis=2,
    ).astype(jnp.bfloat16)
    in_grad = jnp.einsum("thc,thk->hck", by_head, drive_grad, preferred_element_type=jnp.float32)
    input_grad = jnp.einsum(
        "thk,hck->thc", drive_grad, in_proj, preferred_element_type=jnp.float32
    ).reshape(seq_len, local_width)
    input_grad = input_grad + skip_gain * mixed_grad
    trail_rows = from_behind(input_grad[: tap_count - 1], SEQ, -1)
    tail = jnp.concatenate([input_grad, trail_rows], axis=0)
    tokens_grad = conv_taps[0][None, :] * tail[:seq_len]
    for offset in range(1, tap_count):
        tokens_grad = tokens_grad + conv_taps[offset][None, :] * tail[offset : offset + seq_len]
    taps_grad = jnp.stack(
        [
            jnp.sum(
                input_grad * padded[tap_count - 1 - offset : tap_count - 1 - offset + seq_len],
                axis=0,
            )
            for offset in range(tap_count)
        ]
    )
    parts = (out_grad, in_grad, taps_grad)
    packed = tree_sum(jnp.concatenate([p.reshape(-1) for p in parts]), SEQ)
    ends = [0]
    for p in parts:
        ends.append(ends[-1] + p.size)
    out_grad, in_grad, taps_grad = (
        packed[a:b].reshape(p.shape) for a, b, p in zip(ends[:-1], ends[1:], parts)
    )
    return (normed, tokens_grad.astype(jnp.bfloat16), in_grad, out_grad, taps_grad)


def solution(mesh):
    seq_count, chan_count = mesh.devices.shape
    inner = 1
    while inner * inner < seq_count:
        inner *= 2
    devices = mesh.devices.reshape(seq_count // inner, inner, chan_count)
    mesh = Mesh(devices, SEQ + ("chan",))
    in_specs = (
        P(SEQ, "chan"),
        P(None, "chan"),
        P("chan"),
        P("chan"),
        P("chan", None, None),
        P("chan", None, None),
        P("chan"),
        P("chan"),
        P(SEQ),
        P(SEQ, "chan"),
    )
    out_specs = (
        P(SEQ, "chan"),
        P(SEQ, "chan"),
        P("chan", None, None),
        P("chan", None, None),
        P(None, "chan"),
    )
    return jax.shard_map(
        per_device, mesh=mesh, in_specs=in_specs, out_specs=out_specs, check_vma=False
    )
```
